1024 devices in a mesh: gx: 32 (over z, y_lo, core), gy: 32 (over x, y_hi).
Axes of the slice: x: 8, y: 8 (y_hi: 4, y_lo: 2; y = y_hi * 2 + y_lo), z: 8, core: 2. Of those that a mesh axis runs over, the one named last changes fastest.
Arguments:
- load_field: float32 [128, 256, 64, 128], P('gx', 'gy'), may hold values from -6 to 6
- stiffness: float32 [128, 256], P('gx', 'gy'), may hold values from 0.5 to 2
- fault_mask: int32 [128, 256], P('gx', 'gy'), may hold values 0 or 1
- column_operator: float32 [64, 64], replicated
- patch_inverse: bfloat16 [32, 32, 8, 256, 256], P('gx', 'gy')
- patch_anchor: int32 [32, 32, 8], P('gx', 'gy'), may hold values from 0 to 20, as said below
- patch_count: int32 [32, 32], P('gx', 'gy'), may hold values from 1 to 8, as said below
Outputs:
- smoothed: float32 [128, 256, 64, 128], P('gx', 'gy')
The draws below stay inside these ranges and needn't reach their ends.
Inputs may be any that keep to these rules, and one draw needn't show every extreme that they name: `patch_anchor`: the anchors of one device are distinct. `patch_count`: all devices of one gy index below the last, drawn from the seed, have exactly 8 live slots; every other device has at most 4.
All inputs are finite; a program needn't handle non-finite values. No bound on the sum of `fault_mask` on one device may be relied on, other than what follows from the above.
Results may differ from the reference program's by a relative error of at most 0.0027.
Values may be sent and summed in bfloat16 or wider, within the bound.
No kernel may reach another device: no remote copies, remote signals or barrier semaphores. Data moves between devices by JAX's collectives and lax.ppermute only.
A program may use at most 32 MiB of HBM per device.

```python
import math
import jax
import jax.numpy as jnp
from jax import lax

CX = 4
CY = 8
RHS = 128
SLOTS = 8
SWEEPS = 2
COL = 64
PATCH = 256
NX = 128
NY = 256
N_GX = 32
N_GY = 32


def draw_column_operator(key, part):
    first, second = jax.random.split(key)
    diagonal = 2.0 + jax.random.uniform(first, (COL,), jnp.float32)
    spread = jax.random.normal(second, (COL, COL), jnp.float32) * (0.6 / math.sqrt(COL))
    ident = (lax.broadcasted_iota(jnp.int32, (COL, COL), 0) == lax.broadcasted_iota(jnp.int32, (COL, COL), 1)).astype(jnp.float32)
    return ident * diagonal[:, None] + spread


def draw_patch_inverse(key, part):
    first, second = jax.random.split(key)
    shape = (N_GX, N_GY, SLOTS, PATCH, PATCH)
    diagonal = jax.random.uniform(first, (N_GX, N_GY, SLOTS, PATCH, 1), jnp.float32, 0.15, 0.35)
    spread = jax.random.normal(second, shape, jnp.float32) * (0.4 / math.sqrt(PATCH))
    ident = (lax.broadcasted_iota(jnp.int32, (PATCH, PATCH), 0) == lax.broadcasted_iota(jnp.int32, (PATCH, PATCH), 1)).astype(jnp.float32)
    return (ident * diagonal + spread).astype(jnp.bfloat16)


def draw_patch_anchor(key, part):
    keys = jax.random.split(key, N_GX * N_GY)
    orders = jax.vmap(lambda single: jax.random.permutation(single, (CX - 1) * (CY - 1)))(keys)
    return orders[:, :SLOTS].reshape(N_GX, N_GY, SLOTS).astype(jnp.int32)


def draw_patch_count(key, part):
    first, second = jax.random.split(key)
    fault = jax.random.randint(first, (), 0, N_GY - 1)
    drawn = jax.random.randint(second, (N_GX, N_GY), 1, SLOTS // 2 + 1)
    column = lax.broadcasted_iota(jnp.int32, (N_GX, N_GY), 1)
    return jnp.where(column == fault, SLOTS, drawn).astype(jnp.int32)


def with_ends(drawn, rng, low, top_value):
    longest = drawn.shape.index(max(drawn.shape))
    spots = []
    for shift in (0, 1):
        where = [jax.random.randint(jax.random.fold_in(rng, axis), (), 0, length) for axis, length in enumerate(drawn.shape)]
        where[longest] = (where[longest] + shift) % drawn.shape[longest]
        spots.append(tuple(where))
    return drawn.at[spots[0]].set(low).at[spots[1]].set(top_value)


def level_of(rng, extent, pieces, low, largest):
    factor_of, own = 1.0, jax.random.fold_in(rng, 6)
    for axis_at, blocks in pieces:
        heights = jnp.exp(jax.random.uniform(jax.random.fold_in(own, axis_at), (blocks,), jnp.float32, low / len(pieces), largest / len(pieces)))
        factor_of = factor_of * jnp.repeat(heights, extent[axis_at] // blocks).reshape([-1 if axis == axis_at else 1 for axis in range(len(extent))])
    return factor_of


def bell_draw(rng, extent, deviation, limit, shards=(), held_as=jnp.bfloat16):
    level = level_of(rng, extent, shards, -0.22, 0.18) if shards else 1.0
    entries = jax.random.normal(rng, extent, jnp.float32) * deviation * level
    return jnp.minimum(jnp.maximum(entries, -limit), limit).astype(held_as)


def setup_inputs(seed: int = 0) -> dict:
    seeds = jax.random.split(jax.random.key(seed), 8)
    return {
        "load_field": bell_draw(seeds[0], (NX, NY, COL, RHS), 1.0, 6.0, ((0, 32), (1, 32)), jnp.float32),
        "stiffness": jnp.clip(jnp.exp(math.log(2.0) - 1.3862944 * jax.random.uniform(seeds[1], (NX, NY), jnp.float32) ** level_of(seeds[1], (NX, NY), ((0, 32), (1, 32)), -0.2, 0.2)), 0.5, 2.0),
        "fault_mask": with_ends((jax.random.randint(seeds[2], (NX, NY), 0, 4) < 1).astype(jnp.int32), jax.random.fold_in(seeds[2], 1), 0, 1),
        "column_operator": draw_column_operator(jax.random.fold_in(seeds[7], 71), 0),
        "patch_inverse": draw_patch_inverse(jax.random.fold_in(seeds[7], 71), 0),
        "patch_anchor": draw_patch_anchor(jax.random.fold_in(seeds[7], 71), 0),
        "patch_count": draw_patch_count(jax.random.fold_in(seeds[7], 71), 0),
    }


damping = 0.5


def apply_operator(field, stiffness, weight, column_operator):
    local = jnp.einsum("kl,xylr->xykr", column_operator, field, precision=lax.Precision.HIGHEST)
    padded = jnp.pad(field, ((1, 1), (1, 1), (0, 0), (0, 0)))
    wide = jnp.pad(weight, 1)
    beside = wide[2:, 1:-1, None, None] * padded[2:, 1:-1]
    beside = beside + wide[:-2, 1:-1, None, None] * padded[:-2, 1:-1]
    beside = beside + wide[1:-1, 2:, None, None] * padded[1:-1, 2:]
    beside = beside + wide[1:-1, :-2, None, None] * padded[1:-1, :-2]
    return stiffness[:, :, None, None] * local - weight[:, :, None, None] * beside


def device_delta(items):
    packed, inverse, anchors, count = items
    delta = jnp.zeros(packed.shape, jnp.float32)
    zero = jnp.int32(0)
    for number in range(SLOTS):
        anchor = anchors[number].astype(jnp.int32)
        row = (anchor // (CY - 1)).astype(jnp.int32)
        column = (anchor % (CY - 1)).astype(jnp.int32)
        piece = lax.dynamic_slice(packed, (row, column, zero, zero), (2, 2, COL, RHS)).reshape(PATCH, RHS)
        term = damping * jnp.dot(inverse[number].astype(jnp.float32), piece.astype(jnp.float32))
        term = jnp.where(number < count, term, jnp.zeros_like(term))
        current = lax.dynamic_slice(delta, (row, column, zero, zero), (2, 2, COL, RHS))
        delta = lax.dynamic_update_slice(delta, current + term.reshape(2, 2, COL, RHS), (row, column, zero, zero))
    return delta


def reference(load_field, stiffness, fault_mask, column_operator, patch_inverse, patch_anchor, patch_count):
    weight = 1.0 - 0.6 * fault_mask.astype(jnp.float32)
    field = jnp.zeros(load_field.shape, jnp.float32)
    devices = N_GX * N_GY
    inverses = patch_inverse.reshape(devices, SLOTS, PATCH, PATCH)
    anchors = patch_anchor.reshape(devices, SLOTS)
    counts = patch_count.reshape(devices)
    for sweep in range(SWEEPS):
        residual = load_field - apply_operator(field, stiffness, weight, column_operator)
        packed = residual.astype(jnp.bfloat16)
        blocks = packed.reshape(N_GX, CX, N_GY, CY, COL, RHS).transpose(0, 2, 1, 3, 4, 5).reshape(devices, CX, CY, COL, RHS)
        deltas = lax.map(device_delta, (blocks, inverses, anchors, counts))
        delta = deltas.reshape(N_GX, N_GY, CX, CY, COL, RHS).transpose(0, 2, 1, 3, 4, 5).reshape(NX, NY, COL, RHS)
        field = field + delta
    return field
```

```python
import jax
import jax.numpy as jnp
from jax import lax
from jax.experimental import pallas as pl
from jax.experimental.pallas import tpu as pltpu
from jax.sharding import PartitionSpec as P

SWEEPS = 2


damping = 0.5


def patch_kernel(anchor_ref, count_ref, src_ref, inv_ref, *rest):
    if len(rest) == 3:
        base_ref, out_ref, acc_ref = rest
    else:
        base_ref = None
        out_ref, acc_ref = rest
    rows, columns, depth, loads = src_ref.shape
    slots = inv_ref.shape[0]
    count = count_ref[0]
    acc_ref[...] = jnp.zeros(acc_ref.shape, jnp.float32)
    for number in range(slots):

        @pl.when(number < count)
        def _():
            anchor = anchor_ref[number]
            row = anchor // (columns - 1)
            column = anchor % (columns - 1)
            pieces = [
                src_ref[row + i, column + j].astype(jnp.bfloat16)
                for i in range(2)
                for j in range(2)
            ]
            piece = jnp.concatenate(pieces, axis=0)
            term = damping * jnp.dot(
                inv_ref[number], piece, preferred_element_type=jnp.float32
            )
            for k in range(4):
                i, j = divmod(k, 2)
                acc_ref[row + i, column + j] += term[k * depth : (k + 1) * depth]

    if base_ref is None:
        out_ref[...] = acc_ref[...]
    else:
        out_ref[...] = base_ref[...] + acc_ref[...]


def patches(src, inverse, anchors, count, base=None):
    smem = pl.BlockSpec(memory_space=pltpu.SMEM)
    vmem = pl.BlockSpec(memory_space=pltpu.VMEM)
    operands = [anchors, count.reshape(1), src, inverse]
    if base is not None:
        operands.append(base)
    return pl.pallas_call(
        patch_kernel,
        out_shape=jax.ShapeDtypeStruct(src.shape, jnp.float32),
        in_specs=[smem, smem] + [vmem] * (len(operands) - 2),
        out_specs=vmem,
        scratch_shapes=[pltpu.VMEM(src.shape, jnp.float32)],
    )(*operands)


def shifted_in(edge, axis, forward):
    count = lax.axis_size(axis)
    if forward:
        pairs = [(i, i + 1) for i in range(count - 1)]
    else:
        pairs = [(i + 1, i) for i in range(count - 1)]
    return lax.ppermute(edge, axis, pairs)


def per_device(
    load_field, stiffness, fault_mask, column_operator, patch_inverse, patch_anchor, patch_count
):
    weight = 1.0 - 0.6 * fault_mask.astype(jnp.float32)
    inverse = patch_inverse[0, 0]
    anchors = patch_anchor[0, 0]
    count = patch_count[0, 0]

    def residual_of(field):
        weighted = weight[:, :, None, None] * field
        above = shifted_in(weighted[-1:], "gx", True)
        below = shifted_in(weighted[:1], "gx", False)
        left = shifted_in(weighted[:, -1:], "gy", True)
        right = shifted_in(weighted[:, :1], "gy", False)
        local = jnp.einsum("kl,xylr->xykr", column_operator, field, precision=lax.Precision.HIGHEST)
        next_x = jnp.concatenate([weighted[1:], below], axis=0)
        prev_x = jnp.concatenate([above, weighted[:-1]], axis=0)
        next_y = jnp.concatenate([weighted[:, 1:], right], axis=1)
        prev_y = jnp.concatenate([left, weighted[:, :-1]], axis=1)
        beside = next_x + prev_x + next_y + prev_y
        return load_field - (
            stiffness[:, :, None, None] * local - weight[:, :, None, None] * beside
        )

    field = patches(load_field, inverse, anchors, count)
    for sweep in range(1, SWEEPS):
        packed = residual_of(field).astype(jnp.bfloat16)
        field = patches(packed, inverse, anchors, count, base=field)
    return field


def solution(mesh):
    return jax.shard_map(
        per_device,
        mesh=mesh,
        in_specs=(
            P("gx", "gy", None, None),
            P("gx", "gy"),
            P("gx", "gy"),
            P(),
            P("gx", "gy", None, None, None),
            P("gx", "gy", None),
            P("gx", "gy"),
        ),
        out_specs=P("gx", "gy", None, None),
        check_vma=False,
    )
```

```python
import jax
import jax.numpy as jnp
from jax import lax
from jax.experimental import pallas as pl
from jax.experimental.pallas import tpu as pltpu
from jax.sharding import PartitionSpec as P

SWEEPS = 2


damping = 0.5


def deposit_patches(anchor_ref, count_ref, src_ref, inv_ref, acc_ref):
    rows, columns, depth, loads = src_ref.shape
    slots = inv_ref.shape[0]
    count = count_ref[0]
    acc_ref[...] = jnp.zeros(acc_ref.shape, jnp.float32)
    for number in range(slots):

        @pl.when(number < count)
        def _():
            anchor = anchor_ref[number]
            row = anchor // (columns - 1)
            column = anchor % (columns - 1)
            pieces = [
                src_ref[row + i, column + j].astype(jnp.bfloat16)
                for i in range(2)
                for j in range(2)
            ]
            piece = jnp.concatenate(pieces, axis=0)
            term = damping * jnp.dot(
                inv_ref[number], piece, preferred_element_type=jnp.float32
            )
            for k in range(4):
                i, j = divmod(k, 2)
                acc_ref[row + i, column + j] += term[k * depth : (k + 1) * depth]


def first_sweep_kernel(
    anchor_ref, count_ref, weight_ref, src_ref, inv_ref,
    out_ref, top_ref, bottom_ref, left_ref, right_ref, acc_ref,
):
    rows, columns = src_ref.shape[:2]
    deposit_patches(anchor_ref, count_ref, src_ref, inv_ref, acc_ref)
    out_ref[...] = acc_ref[...]
    for y in range(columns):
        top_ref[0, y] = weight_ref[0, y] * acc_ref[0, y]
        bottom_ref[0, y] = weight_ref[rows - 1, y] * acc_ref[rows - 1, y]
    for x in range(rows):
        left_ref[x, 0] = weight_ref[x, 0] * acc_ref[x, 0]
        right_ref[x, 0] = weight_ref[x, columns - 1] * acc_ref[x, columns - 1]


def later_sweep_kernel(
    anchor_ref, count_ref, weight_ref, pre_ref, field_ref, above_ref, below_ref,
    left_ref, right_ref, inv_ref, out_ref, packed_ref, acc_ref,
):
    rows, columns = field_ref.shape[:2]

    def weighted(x, y):
        return weight_ref[x, y] * field_ref[x, y]

    for x in range(rows):
        for y in range(columns):
            next_x = weighted(x + 1, y) if x + 1 < rows else below_ref[0, y]
            prev_x = weighted(x - 1, y) if x > 0 else above_ref[0, y]
            next_y = weighted(x, y + 1) if y + 1 < columns else right_ref[x, 0]
            prev_y = weighted(x, y - 1) if y > 0 else left_ref[x, 0]
            beside = next_x + prev_x + next_y + prev_y
            packed_ref[x, y] = (pre_ref[x, y] + weight_ref[x, y] * beside).astype(
                jnp.bfloat16
            )
    deposit_patches(anchor_ref, count_ref, packed_ref, inv_ref, acc_ref)
    out_ref[...] = field_ref[...] + acc_ref[...]


SMEM = pl.BlockSpec(memory_space=pltpu.SMEM)
VMEM = pl.BlockSpec(memory_space=pltpu.VMEM)


def first_sweep(src, inverse, anchors, count, weight):
    rows, columns, depth, loads = src.shape
    row_edge = jax.ShapeDtypeStruct((1, columns, depth, loads), jnp.float32)
    column_edge = jax.ShapeDtypeStruct((rows, 1, depth, loads), jnp.float32)
    return pl.pallas_call(
        first_sweep_kernel,
        out_shape=(
            jax.ShapeDtypeStruct(src.shape, jnp.float32),
            row_edge, row_edge, column_edge, column_edge,
        ),
        in_specs=[SMEM, SMEM, SMEM, VMEM, VMEM],
        out_specs=(VMEM,) * 5,
        scratch_shapes=[pltpu.VMEM(src.shape, jnp.float32)],
    )(anchors, count.reshape(1), weight, src, inverse)


def later_sweep(pre, field, halos, inverse, anchors, count, weight):
    return pl.pallas_call(
        later_sweep_kernel,
        out_shape=jax.ShapeDtypeStruct(field.shape, jnp.float32),
        in_specs=[SMEM, SMEM, SMEM] + [VMEM] * 7,
        out_specs=VMEM,
        scratch_shapes=[
            pltpu.VMEM(field.shape, jnp.bfloat16),
            pltpu.VMEM(field.shape, jnp.float32),
        ],
    )(anchors, count.reshape(1), weight, pre, field, *halos, inverse)


def shifted_in(edge, axis, forward):
    count = lax.axis_size(axis)
    if forward:
        pairs = [(i, i + 1) for i in range(count - 1)]
    else:
        pairs = [(i + 1, i) for i in range(count - 1)]
    return lax.ppermute(edge, axis, pairs)


def per_device(
    load_field, stiffness, fault_mask, column_operator, patch_inverse, patch_anchor, patch_count
):
    weight = 1.0 - 0.6 * fault_mask.astype(jnp.float32)
    inverse = patch_inverse[0, 0]
    anchors = patch_anchor[0, 0]
    count = patch_count[0, 0]

    field, top, bottom, left, right = first_sweep(load_field, inverse, anchors, count, weight)
    if SWEEPS == 2:
        halos = (
            shifted_in(bottom, "gx", True),
            shifted_in(top, "gx", False),
            shifted_in(right, "gy", True),
            shifted_in(left, "gy", False),
        )
        local = jnp.einsum(
            "kl,xylr->xykr", column_operator, field, precision=lax.Precision.HIGHEST
        )
        pre = load_field - stiffness[:, :, None, None] * local
        field = later_sweep(pre, field, halos, inverse, anchors, count, weight)
    return field


def solution(mesh):
    return jax.shard_map(
        per_device,
        mesh=mesh,
        in_specs=(
            P("gx", "gy", None, None),
            P("gx", "gy"),
            P("gx", "gy"),
            P(),
            P("gx", "gy", None, None, None),
            P("gx", "gy", None),
            P("gx", "gy"),
        ),
        out_specs=P("gx", "gy", None, None),
        check_vma=False,
    )
```

```python
import jax
import jax.numpy as jnp
from jax import lax
from jax.experimental import pallas as pl
from jax.experimental.pallas import tpu as pltpu
from jax.sharding import PartitionSpec as P

SWEEPS = 2


damping = 0.5


def weight_of(mask_ref, x, y):
    return 1.0 - 0.6 * mask_ref[x, y].astype(jnp.float32)


def slot_copies(inv_hbm, inv_ref, sems, count):
    copies = [
        pltpu.make_async_copy(inv_hbm.at[number], inv_ref.at[number], sems.at[number])
        for number in range(inv_ref.shape[0])
    ]
    for number, copy in enumerate(copies):

        @pl.when(number < count)
        def _():
            copy.start()

    return copies


def deposit_patches(anchor_ref, count, src_ref, inv_ref, copies, acc_ref):
    rows, columns, depth, loads = src_ref.shape
    acc_ref[...] = jnp.zeros(acc_ref.shape, jnp.float32)
    for number, copy in enumerate(copies):

        @pl.when(number < count)
        def _():
            anchor = anchor_ref[number]
            row = anchor // (columns - 1)
            column = anchor % (columns - 1)
            pieces = [
                src_ref[row + i, column + j].astype(jnp.bfloat16)
                for i in range(2)
                for j in range(2)
            ]
            piece = jnp.concatenate(pieces, axis=0)
            copy.wait()
            term = damping * jnp.dot(
                inv_ref[number], piece, preferred_element_type=jnp.float32
            )
            for k in range(4):
                i, j = divmod(k, 2)
                acc_ref[row + i, column + j] += term[k * depth : (k + 1) * depth]


def first_sweep_kernel(
    anchor_ref, count_ref, mask_ref, src_ref, inv_hbm,
    out_ref, top_ref, bottom_ref, left_ref, right_ref, inv_ref, sems, acc_ref,
):
    rows, columns = src_ref.shape[:2]
    count = count_ref[0]
    copies = slot_copies(inv_hbm, inv_ref, sems, count)
    deposit_patches(anchor_ref, count, src_ref, inv_ref, copies, acc_ref)
    out_ref[...] = acc_ref[...]
    for y in range(columns):
        top_ref[0, y] = weight_of(mask_ref, 0, y) * acc_ref[0, y]
        bottom_ref[0, y] = weight_of(mask_ref, rows - 1, y) * acc_ref[rows - 1, y]
    for x in range(rows):
        left_ref[x, 0] = weight_of(mask_ref, x, 0) * acc_ref[x, 0]
        right_ref[x, 0] = weight_of(mask_ref, x, columns - 1) * acc_ref[x, columns - 1]


def later_sweep_kernel(
    anchor_ref, count_ref, mask_ref, pre_ref, field_ref, above_hbm, below_hbm,
    left_hbm, right_hbm, inv_hbm, out_ref, above_ref, below_ref, left_ref, right_ref,
    inv_ref, halo_sems, sems, packed_ref, acc_ref,
):
    rows, columns = field_ref.shape[:2]
    count = count_ref[0]
    copies = slot_copies(inv_hbm, inv_ref, sems, count)
    halo_copies = [
        pltpu.make_async_copy(source, target, halo_sems.at[number])
        for number, (source, target) in enumerate(
            [
                (above_hbm, above_ref),
                (below_hbm, below_ref),
                (left_hbm, left_ref),
                (right_hbm, right_ref),
            ]
        )
    ]
    for copy in halo_copies:
        copy.start()

    def weighted(x, y):
        return weight_of(mask_ref, x, y) * field_ref[x, y]

    def residual(x, y):
        next_x = weighted(x + 1, y) if x + 1 < rows else below_ref[0, y]
        prev_x = weighted(x - 1, y) if x > 0 else above_ref[0, y]
        next_y = weighted(x, y + 1) if y + 1 < columns else right_ref[x, 0]
        prev_y = weighted(x, y - 1) if y > 0 else left_ref[x, 0]
        beside = next_x + prev_x + next_y + prev_y
        packed_ref[x, y] = (pre_ref[x, y] + weight_of(mask_ref, x, y) * beside).astype(
            jnp.bfloat16
        )

    vertices = [(x, y) for x in range(rows) for y in range(columns)]
    inner = [(x, y) for x, y in vertices if 0 < x < rows - 1 and 0 < y < columns - 1]
    for x, y in inner:
        residual(x, y)
    for copy in halo_copies:
        copy.wait()
    for x, y in vertices:
        if (x, y) not in inner:
            residual(x, y)
    deposit_patches(anchor_ref, count, packed_ref, inv_ref, copies, acc_ref)
    out_ref[...] = field_ref[...] + acc_ref[...]


SMEM = pl.BlockSpec(memory_space=pltpu.SMEM)
VMEM = pl.BlockSpec(memory_space=pltpu.VMEM)
ANY = pl.BlockSpec(memory_space=pl.ANY)


def first_sweep(src, inverse, anchors, count, mask):
    rows, columns, depth, loads = src.shape
    row_edge = jax.ShapeDtypeStruct((1, columns, depth, loads), jnp.float32)
    column_edge = jax.ShapeDtypeStruct((rows, 1, depth, loads), jnp.float32)
    return pl.pallas_call(
        first_sweep_kernel,
        out_shape=(
            jax.ShapeDtypeStruct(src.shape, jnp.float32),
            row_edge, row_edge, column_edge, column_edge,
        ),
        in_specs=[SMEM, SMEM, SMEM, VMEM, ANY],
        out_specs=(VMEM,) * 5,
        scratch_shapes=[
            pltpu.VMEM(inverse.shape, inverse.dtype),
            pltpu.SemaphoreType.DMA((inverse.shape[0],)),
            pltpu.VMEM(src.shape, jnp.float32),
        ],
    )(anchors, count.reshape(1), mask, src, inverse)


def later_sweep(pre, field, halos, inverse, anchors, count, mask):
    return pl.pallas_call(
        later_sweep_kernel,
        out_shape=jax.ShapeDtypeStruct(field.shape, jnp.float32),
        in_specs=[SMEM, SMEM, SMEM, VMEM, VMEM] + [ANY] * 5,
        out_specs=VMEM,
        scratch_shapes=[pltpu.VMEM(h.shape, h.dtype) for h in halos]
        + [
            pltpu.VMEM(inverse.shape, inverse.dtype),
            pltpu.SemaphoreType.DMA((4,)),
            pltpu.SemaphoreType.DMA((inverse.shape[0],)),
            pltpu.VMEM(field.shape, jnp.bfloat16),
            pltpu.VMEM(field.shape, jnp.float32),
        ],
    )(anchors, count.reshape(1), mask, pre, field, *halos, inverse)


def shifted_in(edge, axis, forward):
    count = lax.axis_size(axis)
    if forward:
        pairs = [(i, i + 1) for i in range(count - 1)]
    else:
        pairs = [(i + 1, i) for i in range(count - 1)]
    return lax.ppermute(edge, axis, pairs)


def per_device(
    load_field, stiffness, fault_mask, column_operator, patch_inverse, patch_anchor, patch_count
):
    inverse = patch_inverse[0, 0]
    anchors = patch_anchor[0, 0]
    count = patch_count[0, 0]

    field, top, bottom, left, right = first_sweep(load_field, inverse, anchors, count, fault_mask)
    if SWEEPS == 2:
        halos = (
            shifted_in(bottom, "gx", True),
            shifted_in(top, "gx", False),
            shifted_in(right, "gy", True),
            shifted_in(left, "gy", False),
        )
        local = jnp.einsum(
            "kl,xylr->xykr", column_operator, field, precision=lax.Precision.HIGHEST
        )
        pre = load_field - stiffness[:, :, None, None] * local
        field = later_sweep(pre, field, halos, inverse, anchors, count, fault_mask)
    return field


def solution(mesh):
    return jax.shard_map(
        per_device,
        mesh=mesh,
        in_specs=(
            P("gx", "gy", None, None),
            P("gx", "gy"),
            P("gx", "gy"),
            P(),
            P("gx", "gy", None, None, None),
            P("gx", "gy", None),
            P("gx", "gy"),
        ),
        out_specs=P("gx", "gy", None, None),
        check_vma=False,
    )
```

```python
import jax
import jax.numpy as jnp
from jax import lax
from jax.experimental import pallas as pl
from jax.experimental.pallas import tpu as pltpu
from jax.sharding import PartitionSpec as P

SWEEPS = 2


damping = 0.5


def weight_of(mask_ref, x, y):
    return 1.0 - 0.6 * mask_ref[x, y].astype(jnp.float32)


def deposit_patches(anchor_ref, count_ref, src_ref, inv_ref, acc_ref):
    rows, columns, depth, loads = src_ref.shape
    slots = inv_ref.shape[0]
    count = count_ref[0]
    acc_ref[...] = jnp.zeros(acc_ref.shape, jnp.float32)
    for number in range(slots):

        @pl.when(number < count)
        def _():
            anchor = anchor_ref[number]
            row = anchor // (columns - 1)
            column = anchor % (columns - 1)
            pieces = [
                src_ref[row + i, column + j].astype(jnp.bfloat16)
                for i in range(2)
                for j in range(2)
            ]
            piece = jnp.concatenate(pieces, axis=0)
            term = damping * jnp.dot(
                inv_ref[number], piece, preferred_element_type=jnp.float32
            )
            for k in range(4):
                i, j = divmod(k, 2)
                acc_ref[row + i, column + j] += term[k * depth : (k + 1) * depth]


def first_sweep_kernel(
    anchor_ref, count_ref, mask_ref, src_ref, inv_ref,
    out_ref, top_ref, bottom_ref, left_ref, right_ref, acc_ref,
):
    rows, columns = src_ref.shape[:2]
    deposit_patches(anchor_ref, count_ref, src_ref, inv_ref, acc_ref)
    out_ref[...] = acc_ref[...]
    for y in range(columns):
        top_ref[0, y] = (weight_of(mask_ref, 0, y) * acc_ref[0, y]).astype(top_ref.dtype)
        bottom_ref[0, y] = (weight_of(mask_ref, rows - 1, y) * acc_ref[rows - 1, y]).astype(bottom_ref.dtype)
    for x in range(rows):
        left_ref[x, 0] = (weight_of(mask_ref, x, 0) * acc_ref[x, 0]).astype(left_ref.dtype)
        right_ref[x, 0] = (weight_of(mask_ref, x, columns - 1) * acc_ref[x, columns - 1]).astype(right_ref.dtype)


def later_sweep_kernel(
    anchor_ref, count_ref, mask_ref, pre_ref, field_ref, above_ref, below_ref,
    left_ref, right_ref, inv_ref, out_ref, packed_ref, acc_ref,
):
    rows, columns = field_ref.shape[:2]

    def weighted(x, y):
        return weight_of(mask_ref, x, y) * field_ref[x, y]

    for x in range(rows):
        for y in range(columns):
            next_x = weighted(x + 1, y) if x + 1 < rows else below_ref[0, y].astype(jnp.float32)
            prev_x = weighted(x - 1, y) if x > 0 else above_ref[0, y].astype(jnp.float32)
            next_y = weighted(x, y + 1) if y + 1 < columns else right_ref[x, 0].astype(jnp.float32)
            prev_y = weighted(x, y - 1) if y > 0 else left_ref[x, 0].astype(jnp.float32)
            beside = next_x + prev_x + next_y + prev_y
            packed_ref[x, y] = (pre_ref[x, y] + weight_of(mask_ref, x, y) * beside).astype(
                jnp.bfloat16
            )
    deposit_patches(anchor_ref, count_ref, packed_ref, inv_ref, acc_ref)
    out_ref[...] = field_ref[...] + acc_ref[...]


SMEM = pl.BlockSpec(memory_space=pltpu.SMEM)
VMEM = pl.BlockSpec(memory_space=pltpu.VMEM)


def first_sweep(src, inverse, anchors, count, mask):
    rows, columns, depth, loads = src.shape
    row_edge = jax.ShapeDtypeStruct((1, columns, depth, loads), jnp.bfloat16)
    column_edge = jax.ShapeDtypeStruct((rows, 1, depth, loads), jnp.bfloat16)
    return pl.pallas_call(
        first_sweep_kernel,
        out_shape=(
            jax.ShapeDtypeStruct(src.shape, jnp.float32),
            row_edge, row_edge, column_edge, column_edge,
        ),
        in_specs=[SMEM, SMEM, SMEM, VMEM, VMEM],
        out_specs=(VMEM,) * 5,
        scratch_shapes=[pltpu.VMEM(src.shape, jnp.float32)],
    )(anchors, count.reshape(1), mask, src, inverse)


def later_sweep(pre, field, halos, inverse, anchors, count, mask):
    return pl.pallas_call(
        later_sweep_kernel,
        out_shape=jax.ShapeDtypeStruct(field.shape, jnp.float32),
        in_specs=[SMEM, SMEM, SMEM] + [VMEM] * 7,
        out_specs=VMEM,
        scratch_shapes=[
            pltpu.VMEM(field.shape, jnp.bfloat16),
            pltpu.VMEM(field.shape, jnp.float32),
        ],
    )(anchors, count.reshape(1), mask, pre, field, *halos, inverse)


def shifted_in(edge, axis, forward):
    count = lax.axis_size(axis)
    if forward:
        pairs = [(i, i + 1) for i in range(count - 1)]
    else:
        pairs = [(i + 1, i) for i in range(count - 1)]
    return lax.ppermute(edge, axis, pairs)


def per_device(
    load_field, stiffness, fault_mask, column_operator, patch_inverse, patch_anchor, patch_count
):
    inverse = patch_inverse[0, 0]
    anchors = patch_anchor[0, 0]
    count = patch_count[0, 0]

    field, top, bottom, left, right = first_sweep(load_field, inverse, anchors, count, fault_mask)
    if SWEEPS == 2:
        halos = (
            shifted_in(bottom, "gx", True),
            shifted_in(top, "gx", False),
            shifted_in(right, "gy", True),
            shifted_in(left, "gy", False),
        )
        local = jnp.einsum(
            "kl,xylr->xykr", column_operator, field, precision=lax.Precision.HIGHEST
        )
        pre = load_field - stiffness[:, :, None, None] * local
        field = later_sweep(pre, field, halos, inverse, anchors, count, fault_mask)
    return field


def solution(mesh):
    return jax.shard_map(
        per_device,
        mesh=mesh,
        in_specs=(
            P("gx", "gy", None, None),
            P("gx", "gy"),
            P("gx", "gy"),
            P(),
            P("gx", "gy", None, None, None),
            P("gx", "gy", None),
            P("gx", "gy"),
        ),
        out_specs=P("gx", "gy", None, None),
        check_vma=False,
    )
```

```python
import jax
import jax.numpy as jnp
from jax import lax
from jax.experimental import pallas as pl
from jax.experimental.pallas import tpu as pltpu
from jax.sharding import PartitionSpec as P

SWEEPS = 2


damping = 0.5


def weight_of(mask_ref, x, y):
    return 1.0 - 0.6 * mask_ref[x, y].astype(jnp.float32)


def deposit_patches(anchor_ref, count_ref, src_ref, inv_ref, acc_ref):
    rows, columns, depth, loads = src_ref.shape
    slots = inv_ref.shape[0]
    count = count_ref[0]
    acc_ref[...] = jnp.zeros(acc_ref.shape, jnp.float32)
    for number in range(slots):

        @pl.when(number < count)
        def _():
            anchor = anchor_ref[number]
            row = anchor // (columns - 1)
            column = anchor % (columns - 1)
            pieces = [
                src_ref[row + i, column + j].astype(jnp.bfloat16)
                for i in range(2)
                for j in range(2)
            ]
            piece = jnp.concatenate(pieces, axis=0)
            term = damping * jnp.dot(
                inv_ref[number], piece, preferred_element_type=jnp.float32
            )
            for k in range(4):
                i, j = divmod(k, 2)
                acc_ref[row + i, column + j] += term[k * depth : (k + 1) * depth]


def first_sweep_kernel(
    anchor_ref, count_ref, mask_ref, src_ref, inv_ref,
    out_ref, top_ref, bottom_ref, left_ref, right_ref, acc_ref,
):
    rows, columns = src_ref.shape[:2]
    deposit_patches(anchor_ref, count_ref, src_ref, inv_ref, acc_ref)
    out_ref[...] = acc_ref[...]
    for y in range(columns):
        top_ref[0, y] = (weight_of(mask_ref, 0, y) * acc_ref[0, y]).astype(top_ref.dtype)
        bottom_ref[0, y] = (weight_of(mask_ref, rows - 1, y) * acc_ref[rows - 1, y]).astype(bottom_ref.dtype)
    for x in range(rows):
        left_ref[x, 0] = (weight_of(mask_ref, x, 0) * acc_ref[x, 0]).astype(left_ref.dtype)
        right_ref[x, 0] = (weight_of(mask_ref, x, columns - 1) * acc_ref[x, columns - 1]).astype(right_ref.dtype)


def later_sweep_kernel(
    anchor_ref, count_ref, mask_ref, stiffness_ref, load_ref, field_ref, operator_ref,
    above_ref, below_ref, left_ref, right_ref, inv_ref, out_ref, packed_ref, acc_ref,
):
    rows, columns, depth, loads = field_ref.shape
    local = []
    for x in range(rows):
        wide = jnp.concatenate([field_ref[x, y] for y in range(columns)], axis=1)
        local.append(
            jnp.dot(
                operator_ref[...], wide,
                precision=lax.Precision.HIGHEST,
                preferred_element_type=jnp.float32,
            )
        )

    def weighted(x, y):
        return weight_of(mask_ref, x, y) * field_ref[x, y]

    for x in range(rows):
        for y in range(columns):
            next_x = weighted(x + 1, y) if x + 1 < rows else below_ref[0, y].astype(jnp.float32)
            prev_x = weighted(x - 1, y) if x > 0 else above_ref[0, y].astype(jnp.float32)
            next_y = weighted(x, y + 1) if y + 1 < columns else right_ref[x, 0].astype(jnp.float32)
            prev_y = weighted(x, y - 1) if y > 0 else left_ref[x, 0].astype(jnp.float32)
            beside = next_x + prev_x + next_y + prev_y
            operated = stiffness_ref[x, y] * local[x][:, y * loads : (y + 1) * loads]
            packed_ref[x, y] = (
                load_ref[x, y] - (operated - weight_of(mask_ref, x, y) * beside)
            ).astype(jnp.bfloat16)
    deposit_patches(anchor_ref, count_ref, packed_ref, inv_ref, acc_ref)
    out_ref[...] = field_ref[...] + acc_ref[...]


SMEM = pl.BlockSpec(memory_space=pltpu.SMEM)
VMEM = pl.BlockSpec(memory_space=pltpu.VMEM)


def first_sweep(src, inverse, anchors, count, mask):
    rows, columns, depth, loads = src.shape
    row_edge = jax.ShapeDtypeStruct((1, columns, depth, loads), jnp.bfloat16)
    column_edge = jax.ShapeDtypeStruct((rows, 1, depth, loads), jnp.bfloat16)
    return pl.pallas_call(
        first_sweep_kernel,
        out_shape=(
            jax.ShapeDtypeStruct(src.shape, jnp.float32),
            row_edge, row_edge, column_edge, column_edge,
        ),
        in_specs=[SMEM, SMEM, SMEM, VMEM, VMEM],
        out_specs=(VMEM,) * 5,
        scratch_shapes=[pltpu.VMEM(src.shape, jnp.float32)],
    )(anchors, count.reshape(1), mask, src, inverse)


def later_sweep(load, field, operator, stiffness, halos, inverse, anchors, count, mask):
    return pl.pallas_call(
        later_sweep_kernel,
        out_shape=jax.ShapeDtypeStruct(field.shape, jnp.float32),
        in_specs=[SMEM, SMEM, SMEM, SMEM] + [VMEM] * 8,
        out_specs=VMEM,
        scratch_shapes=[
            pltpu.VMEM(field.shape, jnp.bfloat16),
            pltpu.VMEM(field.shape, jnp.float32),
        ],
    )(anchors, count.reshape(1), mask, stiffness, load, field, operator, *halos, inverse)


def shifted_in(edge, axis, forward):
    count = lax.axis_size(axis)
    if forward:
        pairs = [(i, i + 1) for i in range(count - 1)]
    else:
        pairs = [(i + 1, i) for i in range(count - 1)]
    return lax.ppermute(edge, axis, pairs)


def per_device(
    load_field, stiffness, fault_mask, column_operator, patch_inverse, patch_anchor, patch_count
):
    inverse = patch_inverse[0, 0]
    anchors = patch_anchor[0, 0]
    count = patch_count[0, 0]

    field, top, bottom, left, right = first_sweep(load_field, inverse, anchors, count, fault_mask)
    if SWEEPS == 2:
        halos = (
            shifted_in(bottom, "gx", True),
            shifted_in(top, "gx", False),
            shifted_in(right, "gy", True),
            shifted_in(left, "gy", False),
        )
        field = later_sweep(
            load_field, field, column_operator, stiffness, halos, inverse, anchors, count,
            fault_mask,
        )
    return field


def solution(mesh):
    return jax.shard_map(
        per_device,
        mesh=mesh,
        in_specs=(
            P("gx", "gy", None, None),
            P("gx", "gy"),
            P("gx", "gy"),
            P(),
            P("gx", "gy", None, None, None),
            P("gx", "gy", None),
            P("gx", "gy"),
        ),
        out_specs=P("gx", "gy", None, None),
        check_vma=False,
    )
```

```python
import jax
import jax.numpy as jnp
from jax import lax
from jax.experimental import pallas as pl
from jax.experimental.pallas import tpu as pltpu
from jax.sharding import PartitionSpec as P

SWEEPS = 2


damping = 0.5


def weight_of(mask_ref, x, y):
    return 1.0 - 0.6 * mask_ref[x, y].astype(jnp.float32)


def deposit_patches(anchor_ref, count_ref, src_ref, inv_ref, acc_ref):
    rows, columns, depth, loads = src_ref.shape
    slots = inv_ref.shape[0]
    count = count_ref[0]
    acc_ref[...] = jnp.zeros(acc_ref.shape, jnp.float32)
    for number in range(slots):

        @pl.when(number < count)
        def _():
            anchor = anchor_ref[number]
            row = anchor // (columns - 1)
            column = anchor % (columns - 1)
            pieces = [
                src_ref[row + i, column + j].astype(jnp.bfloat16)
                for i in range(2)
                for j in range(2)
            ]
            piece = jnp.concatenate(pieces, axis=0)
            term = damping * jnp.dot(
                inv_ref[number], piece, preferred_element_type=jnp.float32
            )
            for k in range(4):
                i, j = divmod(k, 2)
                acc_ref[row + i, column + j] += term[k * depth : (k + 1) * depth]


def first_sweep_kernel(
    anchor_ref, count_ref, mask_ref, src_ref, inv_ref,
    out_ref, top_ref, bottom_ref, left_ref, right_ref, acc_ref,
):
    rows, columns = src_ref.shape[:2]
    deposit_patches(anchor_ref, count_ref, src_ref, inv_ref, acc_ref)
    out_ref[...] = acc_ref[...]
    for y in range(columns):
        top_ref[0, y] = (weight_of(mask_ref, 0, y) * acc_ref[0, y]).astype(top_ref.dtype)
        bottom_ref[0, y] = (weight_of(mask_ref, rows - 1, y) * acc_ref[rows - 1, y]).astype(bottom_ref.dtype)
    for x in range(rows):
        left_ref[x, 0] = (weight_of(mask_ref, x, 0) * acc_ref[x, 0]).astype(left_ref.dtype)
        right_ref[x, 0] = (weight_of(mask_ref, x, columns - 1) * acc_ref[x, columns - 1]).astype(right_ref.dtype)


def operator_kernel(stiffness_ref, load_ref, field_ref, operator_ref, pre_ref):
    rows, columns, depth, loads = field_ref.shape
    for x in range(rows):
        wide = jnp.concatenate([field_ref[x, y] for y in range(columns)], axis=1)
        local = jnp.dot(
            operator_ref[...], wide,
            precision=lax.Precision.HIGHEST,
            preferred_element_type=jnp.float32,
        )
        for y in range(columns):
            pre_ref[x, y] = load_ref[x, y] - stiffness_ref[x, y] * local[
                :, y * loads : (y + 1) * loads
            ]


def later_sweep_kernel(
    anchor_ref, count_ref, mask_ref, pre_ref, field_ref,
    above_ref, below_ref, left_ref, right_ref, inv_ref, out_ref, packed_ref, acc_ref,
):
    rows, columns = field_ref.shape[:2]

    def weighted(x, y):
        return weight_of(mask_ref, x, y) * field_ref[x, y]

    for x in range(rows):
        for y in range(columns):
            next_x = weighted(x + 1, y) if x + 1 < rows else below_ref[0, y].astype(jnp.float32)
            prev_x = weighted(x - 1, y) if x > 0 else above_ref[0, y].astype(jnp.float32)
            next_y = weighted(x, y + 1) if y + 1 < columns else right_ref[x, 0].astype(jnp.float32)
            prev_y = weighted(x, y - 1) if y > 0 else left_ref[x, 0].astype(jnp.float32)
            beside = next_x + prev_x + next_y + prev_y
            packed_ref[x, y] = (pre_ref[x, y] + weight_of(mask_ref, x, y) * beside).astype(
                jnp.bfloat16
            )
    deposit_patches(anchor_ref, count_ref, packed_ref, inv_ref, acc_ref)
    out_ref[...] = field_ref[...] + acc_ref[...]


SMEM = pl.BlockSpec(memory_space=pltpu.SMEM)
VMEM = pl.BlockSpec(memory_space=pltpu.VMEM)


def first_sweep(src, inverse, anchors, count, mask):
    rows, columns, depth, loads = src.shape
    row_edge = jax.ShapeDtypeStruct((1, columns, depth, loads), jnp.bfloat16)
    column_edge = jax.ShapeDtypeStruct((rows, 1, depth, loads), jnp.bfloat16)
    return pl.pallas_call(
        first_sweep_kernel,
        out_shape=(
            jax.ShapeDtypeStruct(src.shape, jnp.float32),
            row_edge, row_edge, column_edge, column_edge,
        ),
        in_specs=[SMEM, SMEM, SMEM, VMEM, VMEM],
        out_specs=(VMEM,) * 5,
        scratch_shapes=[pltpu.VMEM(src.shape, jnp.float32)],
    )(anchors, count.reshape(1), mask, src, inverse)


def operator_part(load, field, operator, stiffness):
    rows, columns, depth, loads = field.shape
    flops = 2 * rows * columns * depth * depth * loads * 6
    return pl.pallas_call(
        operator_kernel,
        out_shape=jax.ShapeDtypeStruct(field.shape, jnp.float32),
        in_specs=[SMEM, VMEM, VMEM, VMEM],
        out_specs=VMEM,
        cost_estimate=pl.CostEstimate(
            flops=flops, bytes_accessed=3 * field.size * 4, transcendentals=0
        ),
    )(stiffness, load, field, operator)


def later_sweep(pre, field, halos, inverse, anchors, count, mask):
    return pl.pallas_call(
        later_sweep_kernel,
        out_shape=jax.ShapeDtypeStruct(field.shape, jnp.float32),
        in_specs=[SMEM, SMEM, SMEM] + [VMEM] * 7,
        out_specs=VMEM,
        scratch_shapes=[
            pltpu.VMEM(field.shape, jnp.bfloat16),
            pltpu.VMEM(field.shape, jnp.float32),
        ],
    )(anchors, count.reshape(1), mask, pre, field, *halos, inverse)


def shifted_in(edge, axis, forward):
    count = lax.axis_size(axis)
    if forward:
        pairs = [(i, i + 1) for i in range(count - 1)]
    else:
        pairs = [(i + 1, i) for i in range(count - 1)]
    return lax.ppermute(edge, axis, pairs)


def per_device(
    load_field, stiffness, fault_mask, column_operator, patch_inverse, patch_anchor, patch_count
):
    inverse = patch_inverse[0, 0]
    anchors = patch_anchor[0, 0]
    count = patch_count[0, 0]

    field, top, bottom, left, right = first_sweep(load_field, inverse, anchors, count, fault_mask)
    if SWEEPS == 2:
        halos = (
            shifted_in(bottom, "gx", True),
            shifted_in(top, "gx", False),
            shifted_in(right, "gy", True),
            shifted_in(left, "gy", False),
        )
        pre = operator_part(load_field, field, column_operator, stiffness)
        field = later_sweep(pre, field, halos, inverse, anchors, count, fault_mask)
    return field


def solution(mesh):
    return jax.shard_map(
        per_device,
        mesh=mesh,
        in_specs=(
            P("gx", "gy", None, None),
            P("gx", "gy"),
            P("gx", "gy"),
            P(),
            P("gx", "gy", None, None, None),
            P("gx", "gy", None),
            P("gx", "gy"),
        ),
        out_specs=P("gx", "gy", None, None),
        check_vma=False,
    )
```

```python
import jax
import jax.numpy as jnp
from jax import lax
from jax.experimental import pallas as pl
from jax.experimental.pallas import tpu as pltpu
from jax.sharding import PartitionSpec as P

SWEEPS = 2


damping = 0.5


def weight_of(mask_ref, x, y):
    return 1.0 - 0.6 * mask_ref[x, y].astype(jnp.float32)


def deposit_patches(anchor_ref, count_ref, src_ref, inv_ref, acc_ref):
    rows, columns, depth, loads = src_ref.shape
    slots = inv_ref.shape[0]
    count = count_ref[0]
    for number in range(slots):

        @pl.when(number < count)
        def _():
            anchor = anchor_ref[number]
            row = anchor // (columns - 1)
            column = anchor % (columns - 1)
            pieces = [
                src_ref[row + i, column + j].astype(jnp.bfloat16)
                for i in range(2)
                for j in range(2)
            ]
            piece = jnp.concatenate(pieces, axis=0)
            term = damping * jnp.dot(
                inv_ref[number], piece, preferred_element_type=jnp.float32
            )
            for k in range(4):
                i, j = divmod(k, 2)
                acc_ref[row + i, column + j] += term[k * depth : (k + 1) * depth]


def first_sweep_kernel(
    anchor_ref, count_ref, mask_ref, src_ref, inv_ref,
    out_ref, top_ref, bottom_ref, left_ref, right_ref,
):
    rows, columns = src_ref.shape[:2]
    acc_ref = out_ref
    acc_ref[...] = jnp.zeros(acc_ref.shape, jnp.float32)
    deposit_patches(anchor_ref, count_ref, src_ref, inv_ref, acc_ref)
    for y in range(columns):
        top_ref[0, y] = (weight_of(mask_ref, 0, y) * acc_ref[0, y]).astype(top_ref.dtype)
        bottom_ref[0, y] = (weight_of(mask_ref, rows - 1, y) * acc_ref[rows - 1, y]).astype(bottom_ref.dtype)
    for x in range(rows):
        left_ref[x, 0] = (weight_of(mask_ref, x, 0) * acc_ref[x, 0]).astype(left_ref.dtype)
        right_ref[x, 0] = (weight_of(mask_ref, x, columns - 1) * acc_ref[x, columns - 1]).astype(right_ref.dtype)


def operator_kernel(stiffness_ref, load_ref, field_ref, operator_ref, pre_ref):
    rows, columns, depth, loads = field_ref.shape
    for x in range(rows):
        wide = jnp.concatenate([field_ref[x, y] for y in range(columns)], axis=1)
        local = jnp.dot(
            operator_ref[...], wide,
            precision=lax.Precision.HIGHEST,
            preferred_element_type=jnp.float32,
        )
        for y in range(columns):
            pre_ref[x, y] = load_ref[x, y] - stiffness_ref[x, y] * local[
                :, y * loads : (y + 1) * loads
            ]


def later_sweep_kernel(
    anchor_ref, count_ref, mask_ref, pre_ref, field_ref,
    above_ref, below_ref, left_ref, right_ref, inv_ref, out_ref, packed_ref,
):
    rows, columns = field_ref.shape[:2]

    def weighted(x, y):
        return weight_of(mask_ref, x, y) * field_ref[x, y]

    for x in range(rows):
        for y in range(columns):
            next_x = weighted(x + 1, y) if x + 1 < rows else below_ref[0, y].astype(jnp.float32)
            prev_x = weighted(x - 1, y) if x > 0 else above_ref[0, y].astype(jnp.float32)
            next_y = weighted(x, y + 1) if y + 1 < columns else right_ref[x, 0].astype(jnp.float32)
            prev_y = weighted(x, y - 1) if y > 0 else left_ref[x, 0].astype(jnp.float32)
            beside = next_x + prev_x + next_y + prev_y
            packed_ref[x, y] = (pre_ref[x, y] + weight_of(mask_ref, x, y) * beside).astype(
                jnp.bfloat16
            )
    out_ref[...] = field_ref[...]
    deposit_patches(anchor_ref, count_ref, packed_ref, inv_ref, out_ref)


SMEM = pl.BlockSpec(memory_space=pltpu.SMEM)
VMEM = pl.BlockSpec(memory_space=pltpu.VMEM)


def first_sweep(src, inverse, anchors, count, mask):
    rows, columns, depth, loads = src.shape
    row_edge = jax.ShapeDtypeStruct((1, columns, depth, loads), jnp.bfloat16)
    column_edge = jax.ShapeDtypeStruct((rows, 1, depth, loads), jnp.bfloat16)
    return pl.pallas_call(
        first_sweep_kernel,
        out_shape=(
            jax.ShapeDtypeStruct(src.shape, jnp.float32),
            row_edge, row_edge, column_edge, column_edge,
        ),
        in_specs=[SMEM, SMEM, SMEM, VMEM, VMEM],
        out_specs=(VMEM,) * 5,
    )(anchors, count.reshape(1), mask, src, inverse)


def operator_part(load, field, operator, stiffness):
    rows, columns, depth, loads = field.shape
    flops = 2 * rows * columns * depth * depth * loads * 6
    return pl.pallas_call(
        operator_kernel,
        out_shape=jax.ShapeDtypeStruct(field.shape, jnp.float32),
        in_specs=[SMEM, VMEM, VMEM, VMEM],
        out_specs=VMEM,
        cost_estimate=pl.CostEstimate(
            flops=flops, bytes_accessed=3 * field.size * 4, transcendentals=0
        ),
    )(stiffness, load, field, operator)


def later_sweep(pre, field, halos, inverse, anchors, count, mask):
    return pl.pallas_call(
        later_sweep_kernel,
        out_shape=jax.ShapeDtypeStruct(field.shape, jnp.float32),
        in_specs=[SMEM, SMEM, SMEM] + [VMEM] * 7,
        out_specs=VMEM,
        scratch_shapes=[pltpu.VMEM(field.shape, jnp.bfloat16)],
    )(anchors, count.reshape(1), mask, pre, field, *halos, inverse)


def shifted_in(edge, axis, forward):
    count = lax.axis_size(axis)
    if forward:
        pairs = [(i, i + 1) for i in range(count - 1)]
    else:
        pairs = [(i + 1, i) for i in range(count - 1)]
    return lax.ppermute(edge, axis, pairs)


def per_device(
    load_field, stiffness, fault_mask, column_operator, patch_inverse, patch_anchor, patch_count
):
    inverse = patch_inverse[0, 0]
    anchors = patch_anchor[0, 0]
    count = patch_count[0, 0]

    field, top, bottom, left, right = first_sweep(load_field, inverse, anchors, count, fault_mask)
    if SWEEPS == 2:
        halos = (
            shifted_in(bottom, "gx", True),
            shifted_in(top, "gx", False),
            shifted_in(right, "gy", True),
            shifted_in(left, "gy", False),
        )
        pre = operator_part(load_field, field, column_operator, stiffness)
        field = later_sweep(pre, field, halos, inverse, anchors, count, fault_mask)
    return field


def solution(mesh):
    return jax.shard_map(
        per_device,
        mesh=mesh,
        in_specs=(
            P("gx", "gy", None, None),
            P("gx", "gy"),
            P("gx", "gy"),
            P(),
            P("gx", "gy", None, None, None),
            P("gx", "gy", None),
            P("gx", "gy"),
        ),
        out_specs=P("gx", "gy", None, None),
        check_vma=False,
    )
```

```python
import jax
import jax.numpy as jnp
from jax import lax
from jax.experimental import pallas as pl
from jax.experimental.pallas import tpu as pltpu
from jax.sharding import PartitionSpec as P

SWEEPS = 2


damping = 0.5


def weight_of(mask_ref, x, y):
    return 1.0 - 0.6 * mask_ref[x, y].astype(jnp.float32)


def deposit_patches(anchor_ref, count_ref, src_ref, inv_ref, acc_ref):
    rows, columns, depth, loads = src_ref.shape
    slots = inv_ref.shape[0]
    count = count_ref[0]
    for number in range(slots):

        @pl.when(number < count)
        def _():
            anchor = anchor_ref[number]
            row = anchor // (columns - 1)
            column = anchor % (columns - 1)
            pieces = [
                src_ref[row + i, column + j].astype(jnp.bfloat16)
                for i in range(2)
                for j in range(2)
            ]
            piece = jnp.concatenate(pieces, axis=0)
            term = damping * jnp.dot(
                inv_ref[number], piece, preferred_element_type=jnp.float32
            )
            for k in range(4):
                i, j = divmod(k, 2)
                acc_ref[row + i, column + j] += term[k * depth : (k + 1) * depth]


def first_sweep_kernel(
    anchor_ref, count_ref, mask_ref, src_ref, inv_ref,
    out_ref, top_ref, bottom_ref, left_ref, right_ref,
):
    rows, columns = src_ref.shape[:2]
    acc_ref = out_ref
    acc_ref[...] = jnp.zeros(acc_ref.shape, jnp.float32)
    deposit_patches(anchor_ref, count_ref, src_ref, inv_ref, acc_ref)
    for y in range(columns):
        top_ref[0, y] = (weight_of(mask_ref, 0, y) * acc_ref[0, y]).astype(top_ref.dtype)
        bottom_ref[0, y] = (weight_of(mask_ref, rows - 1, y) * acc_ref[rows - 1, y]).astype(bottom_ref.dtype)
    for x in range(rows):
        left_ref[x, 0] = (weight_of(mask_ref, x, 0) * acc_ref[x, 0]).astype(left_ref.dtype)
        right_ref[x, 0] = (weight_of(mask_ref, x, columns - 1) * acc_ref[x, columns - 1]).astype(right_ref.dtype)


def operator_kernel(mask_ref, stiffness_ref, load_ref, field_ref, operator_ref, pre_ref):
    rows, columns, depth, loads = field_ref.shape

    def weighted(x, y):
        return weight_of(mask_ref, x, y) * field_ref[x, y]

    for x in range(rows):
        wide = jnp.concatenate([field_ref[x, y] for y in range(columns)], axis=1)
        local = jnp.dot(
            operator_ref[...], wide,
            precision=lax.Precision.HIGHEST,
            preferred_element_type=jnp.float32,
        )
        for y in range(columns):
            near = [
                weighted(x + dx, y + dy)
                for dx, dy in ((1, 0), (-1, 0), (0, 1), (0, -1))
                if 0 <= x + dx < rows and 0 <= y + dy < columns
            ]
            beside = near[0]
            for term in near[1:]:
                beside = beside + term
            operated = stiffness_ref[x, y] * local[:, y * loads : (y + 1) * loads]
            pre_ref[x, y] = load_ref[x, y] - (operated - weight_of(mask_ref, x, y) * beside)


def later_sweep_kernel(
    anchor_ref, count_ref, mask_ref, pre_ref, field_ref,
    above_ref, below_ref, left_ref, right_ref, inv_ref, out_ref, packed_ref,
):
    rows, columns = field_ref.shape[:2]
    for x in range(rows):
        for y in range(columns):
            outside = []
            if x + 1 == rows:
                outside.append(below_ref[0, y])
            if x == 0:
                outside.append(above_ref[0, y])
            if y + 1 == columns:
                outside.append(right_ref[x, 0])
            if y == 0:
                outside.append(left_ref[x, 0])
            value = pre_ref[x, y]
            if outside:
                halo = outside[0].astype(jnp.float32)
                for term in outside[1:]:
                    halo = halo + term.astype(jnp.float32)
                value = value + weight_of(mask_ref, x, y) * halo
            packed_ref[x, y] = value.astype(jnp.bfloat16)
    out_ref[...] = field_ref[...]
    deposit_patches(anchor_ref, count_ref, packed_ref, inv_ref, out_ref)


SMEM = pl.BlockSpec(memory_space=pltpu.SMEM)
VMEM = pl.BlockSpec(memory_space=pltpu.VMEM)


def first_sweep(src, inverse, anchors, count, mask):
    rows, columns, depth, loads = src.shape
    row_edge = jax.ShapeDtypeStruct((1, columns, depth, loads), jnp.bfloat16)
    column_edge = jax.ShapeDtypeStruct((rows, 1, depth, loads), jnp.bfloat16)
    return pl.pallas_call(
        first_sweep_kernel,
        out_shape=(
            jax.ShapeDtypeStruct(src.shape, jnp.float32),
            row_edge, row_edge, column_edge, column_edge,
        ),
        in_specs=[SMEM, SMEM, SMEM, VMEM, VMEM],
        out_specs=(VMEM,) * 5,
    )(anchors, count.reshape(1), mask, src, inverse)


def operator_part(load, field, operator, stiffness, mask):
    rows, columns, depth, loads = field.shape
    flops = 2 * rows * columns * depth * depth * loads * 6
    return pl.pallas_call(
        operator_kernel,
        out_shape=jax.ShapeDtypeStruct(field.shape, jnp.float32),
        in_specs=[SMEM, SMEM, VMEM, VMEM, VMEM],
        out_specs=VMEM,
        cost_estimate=pl.CostEstimate(
            flops=flops, bytes_accessed=3 * field.size * 4, transcendentals=0
        ),
    )(mask, stiffness, load, field, operator)


def later_sweep(pre, field, halos, inverse, anchors, count, mask):
    return pl.pallas_call(
        later_sweep_kernel,
        out_shape=jax.ShapeDtypeStruct(field.shape, jnp.float32),
        in_specs=[SMEM, SMEM, SMEM] + [VMEM] * 7,
        out_specs=VMEM,
        scratch_shapes=[pltpu.VMEM(field.shape, jnp.bfloat16)],
    )(anchors, count.reshape(1), mask, pre, field, *halos, inverse)


def shifted_in(edge, axis, forward):
    count = lax.axis_size(axis)
    if forward:
        pairs = [(i, i + 1) for i in range(count - 1)]
    else:
        pairs = [(i + 1, i) for i in range(count - 1)]
    return lax.ppermute(edge, axis, pairs)


def per_device(
    load_field, stiffness, fault_mask, column_operator, patch_inverse, patch_anchor, patch_count
):
    inverse = patch_inverse[0, 0]
    anchors = patch_anchor[0, 0]
    count = patch_count[0, 0]

    field, top, bottom, left, right = first_sweep(load_field, inverse, anchors, count, fault_mask)
    if SWEEPS == 2:
        halos = (
            shifted_in(bottom, "gx", True),
            shifted_in(top, "gx", False),
            shifted_in(right, "gy", True),
            shifted_in(left, "gy", False),
        )
        pre = operator_part(load_field, field, column_operator, stiffness, fault_mask)
        field = later_sweep(pre, field, halos, inverse, anchors, count, fault_mask)
    return field


def solution(mesh):
    return jax.shard_map(
        per_device,
        mesh=mesh,
        in_specs=(
            P("gx", "gy", None, None),
            P("gx", "gy"),
            P("gx", "gy"),
            P(),
            P("gx", "gy", None, None, None),
            P("gx", "gy", None),
            P("gx", "gy"),
        ),
        out_specs=P("gx", "gy", None, None),
        check_vma=False,
    )
```

```python
import jax
import jax.numpy as jnp
from jax import lax
from jax.experimental import pallas as pl
from jax.experimental.pallas import tpu as pltpu
from jax.sharding import PartitionSpec as P

SWEEPS = 2


damping = 0.5


def weight_of(mask_ref, x, y):
    return 1.0 - 0.6 * mask_ref[x, y].astype(jnp.float32)


def deposit_patches(anchor_ref, count_ref, src_ref, inv_ref, acc_ref):
    rows, columns, depth, loads = src_ref.shape
    slots = inv_ref.shape[0]
    count = count_ref[0]
    for number in range(slots):

        @pl.when(number < count)
        def _():
            anchor = anchor_ref[number]
            row = anchor // (columns - 1)
            column = anchor % (columns - 1)
            pieces = [
                src_ref[row + i, column + j].astype(jnp.bfloat16)
                for i in range(2)
                for j in range(2)
            ]
            piece = jnp.concatenate(pieces, axis=0)
            term = damping * jnp.dot(
                inv_ref[number], piece, preferred_element_type=jnp.float32
            )
            for k in range(4):
                i, j = divmod(k, 2)
                acc_ref[row + i, column + j] += term[k * depth : (k + 1) * depth]


def first_sweep_kernel(
    anchor_ref, count_ref, mask_ref, src_ref, inv_ref,
    out_ref, top_ref, bottom_ref, left_ref, right_ref,
):
    rows, columns = src_ref.shape[:2]
    acc_ref = out_ref
    acc_ref[...] = jnp.zeros(acc_ref.shape, jnp.float32)
    deposit_patches(anchor_ref, count_ref, src_ref, inv_ref, acc_ref)
    for y in range(columns):
        top_ref[0, y] = (weight_of(mask_ref, 0, y) * acc_ref[0, y]).astype(top_ref.dtype)
        bottom_ref[0, y] = (weight_of(mask_ref, rows - 1, y) * acc_ref[rows - 1, y]).astype(bottom_ref.dtype)
    for x in range(rows):
        left_ref[x, 0] = (weight_of(mask_ref, x, 0) * acc_ref[x, 0]).astype(left_ref.dtype)
        right_ref[x, 0] = (weight_of(mask_ref, x, columns - 1) * acc_ref[x, columns - 1]).astype(right_ref.dtype)


def operator_kernel(mask_ref, stiffness_ref, load_ref, field_ref, operator_ref, pre_ref):
    rows, columns, depth, loads = field_ref.shape

    def weighted(x, y):
        return weight_of(mask_ref, x, y) * field_ref[x, y]

    for x in range(rows):
        wide = jnp.concatenate([field_ref[x, y] for y in range(columns)], axis=1)
        local = jnp.dot(
            operator_ref[...], wide,
            precision=lax.Precision.HIGHEST,
            preferred_element_type=jnp.float32,
        )
        for y in range(columns):
            near = [
                weighted(x + dx, y + dy)
                for dx, dy in ((1, 0), (-1, 0), (0, 1), (0, -1))
                if 0 <= x + dx < rows and 0 <= y + dy < columns
            ]
            beside = near[0]
            for term in near[1:]:
                beside = beside + term
            operated = stiffness_ref[x, y] * local[:, y * loads : (y + 1) * loads]
            pre_ref[x, y] = load_ref[x, y] - (operated - weight_of(mask_ref, x, y) * beside)


def later_sweep_kernel(anchor_ref, count_ref, packed_ref, field_ref, inv_ref, out_ref):
    out_ref[...] = field_ref[...]
    deposit_patches(anchor_ref, count_ref, packed_ref, inv_ref, out_ref)


SMEM = pl.BlockSpec(memory_space=pltpu.SMEM)
VMEM = pl.BlockSpec(memory_space=pltpu.VMEM)


def first_sweep(src, inverse, anchors, count, mask):
    rows, columns, depth, loads = src.shape
    row_edge = jax.ShapeDtypeStruct((1, columns, depth, loads), jnp.bfloat16)
    column_edge = jax.ShapeDtypeStruct((rows, 1, depth, loads), jnp.bfloat16)
    return pl.pallas_call(
        first_sweep_kernel,
        out_shape=(
            jax.ShapeDtypeStruct(src.shape, jnp.float32),
            row_edge, row_edge, column_edge, column_edge,
        ),
        in_specs=[SMEM, SMEM, SMEM, VMEM, VMEM],
        out_specs=(VMEM,) * 5,
    )(anchors, count.reshape(1), mask, src, inverse)


def operator_part(load, field, operator, stiffness, mask):
    rows, columns, depth, loads = field.shape
    flops = 2 * rows * columns * depth * depth * loads * 6
    return pl.pallas_call(
        operator_kernel,
        out_shape=jax.ShapeDtypeStruct(field.shape, jnp.float32),
        in_specs=[SMEM, SMEM, VMEM, VMEM, VMEM],
        out_specs=VMEM,
        cost_estimate=pl.CostEstimate(
            flops=flops, bytes_accessed=3 * field.size * 4, transcendentals=0
        ),
    )(mask, stiffness, load, field, operator)


def later_sweep(packed, field, inverse, anchors, count):
    return pl.pallas_call(
        later_sweep_kernel,
        out_shape=jax.ShapeDtypeStruct(field.shape, jnp.float32),
        in_specs=[SMEM, SMEM, VMEM, VMEM, VMEM],
        out_specs=VMEM,
    )(anchors, count.reshape(1), packed, field, inverse)


def with_halos(pre, halos, mask):
    rows, columns = pre.shape[:2]
    above, below, left, right = (halo.astype(jnp.float32) for halo in halos)
    outside = (
        jnp.pad(below, ((rows - 1, 0), (0, 0), (0, 0), (0, 0)))
        + jnp.pad(above, ((0, rows - 1), (0, 0), (0, 0), (0, 0)))
        + jnp.pad(right, ((0, 0), (columns - 1, 0), (0, 0), (0, 0)))
        + jnp.pad(left, ((0, 0), (0, columns - 1), (0, 0), (0, 0)))
    )
    weight = 1.0 - 0.6 * mask.astype(jnp.float32)
    return (pre + weight[:, :, None, None] * outside).astype(jnp.bfloat16)


def shifted_in(edge, axis, forward):
    count = lax.axis_size(axis)
    if forward:
        pairs = [(i, i + 1) for i in range(count - 1)]
    else:
        pairs = [(i + 1, i) for i in range(count - 1)]
    return lax.ppermute(edge, axis, pairs)


def per_device(
    load_field, stiffness, fault_mask, column_operator, patch_inverse, patch_anchor, patch_count
):
    inverse = patch_inverse[0, 0]
    anchors = patch_anchor[0, 0]
    count = patch_count[0, 0]

    field, top, bottom, left, right = first_sweep(load_field, inverse, anchors, count, fault_mask)
    if SWEEPS == 2:
        halos = (
            shifted_in(bottom, "gx", True),
            shifted_in(top, "gx", False),
            shifted_in(right, "gy", True),
            shifted_in(left, "gy", False),
        )
        pre = operator_part(load_field, field, column_operator, stiffness, fault_mask)
        packed = with_halos(pre, halos, fault_mask)
        field = later_sweep(packed, field, inverse, anchors, count)
    return field


def solution(mesh):
    return jax.shard_map(
        per_device,
        mesh=mesh,
        in_specs=(
            P("gx", "gy", None, None),
            P("gx", "gy"),
            P("gx", "gy"),
            P(),
            P("gx", "gy", None, None, None),
            P("gx", "gy", None),
            P("gx", "gy"),
        ),
        out_specs=P("gx", "gy", None, None),
        check_vma=False,
    )
```

```python
import jax
import jax.numpy as jnp
from jax import lax
from jax.experimental import pallas as pl
from jax.experimental.pallas import tpu as pltpu
from jax.sharding import PartitionSpec as P

SWEEPS = 2


damping = 0.5


def weight_of(mask_ref, x, y):
    return 1.0 - 0.6 * mask_ref[x, y].astype(jnp.float32)


def fetch_inverse(count_ref, inv_hbm, inv_ref, sem):
    slots = inv_ref.shape[0]
    half = slots // 2
    count = count_ref[0]

    @pl.when(count > half)
    def _():
        copy = pltpu.make_async_copy(inv_hbm, inv_ref, sem)
        copy.start()
        copy.wait()

    @pl.when(count <= half)
    def _():
        copy = pltpu.make_async_copy(
            inv_hbm.at[pl.ds(0, half)], inv_ref.at[pl.ds(0, half)], sem
        )
        copy.start()
        copy.wait()


def deposit_patches(anchor_ref, count_ref, src_ref, inv_ref, acc_ref):
    rows, columns, depth, loads = src_ref.shape
    slots = inv_ref.shape[0]
    count = count_ref[0]
    for number in range(slots):

        @pl.when(number < count)
        def _():
            anchor = anchor_ref[number]
            row = anchor // (columns - 1)
            column = anchor % (columns - 1)
            pieces = [
                src_ref[row + i, column + j].astype(jnp.bfloat16)
                for i in range(2)
                for j in range(2)
            ]
            piece = jnp.concatenate(pieces, axis=0)
            term = damping * jnp.dot(
                inv_ref[number], piece, preferred_element_type=jnp.float32
            )
            for k in range(4):
                i, j = divmod(k, 2)
                acc_ref[row + i, column + j] += term[k * depth : (k + 1) * depth]


def first_sweep_kernel(
    anchor_ref, count_ref, mask_ref, src_ref, inv_hbm,
    out_ref, top_ref, bottom_ref, left_ref, right_ref, inv_ref, sem,
):
    rows, columns = src_ref.shape[:2]
    acc_ref = out_ref
    acc_ref[...] = jnp.zeros(acc_ref.shape, jnp.float32)
    fetch_inverse(count_ref, inv_hbm, inv_ref, sem)
    deposit_patches(anchor_ref, count_ref, src_ref, inv_ref, acc_ref)
    for y in range(columns):
        top_ref[0, y] = (weight_of(mask_ref, 0, y) * acc_ref[0, y]).astype(top_ref.dtype)
        bottom_ref[0, y] = (weight_of(mask_ref, rows - 1, y) * acc_ref[rows - 1, y]).astype(bottom_ref.dtype)
    for x in range(rows):
        left_ref[x, 0] = (weight_of(mask_ref, x, 0) * acc_ref[x, 0]).astype(left_ref.dtype)
        right_ref[x, 0] = (weight_of(mask_ref, x, columns - 1) * acc_ref[x, columns - 1]).astype(right_ref.dtype)


def operator_kernel(mask_ref, stiffness_ref, load_ref, field_ref, operator_ref, pre_ref):
    rows, columns, depth, loads = field_ref.shape

    def weighted(x, y):
        return weight_of(mask_ref, x, y) * field_ref[x, y]

    for x in range(rows):
        wide = jnp.concatenate([field_ref[x, y] for y in range(columns)], axis=1)
        local = jnp.dot(
            operator_ref[...], wide,
            precision=lax.Precision.HIGHEST,
            preferred_element_type=jnp.float32,
        )
        for y in range(columns):
            near = [
                weighted(x + dx, y + dy)
                for dx, dy in ((1, 0), (-1, 0), (0, 1), (0, -1))
                if 0 <= x + dx < rows and 0 <= y + dy < columns
            ]
            beside = near[0]
            for term in near[1:]:
                beside = beside + term
            operated = stiffness_ref[x, y] * local[:, y * loads : (y + 1) * loads]
            pre_ref[x, y] = load_ref[x, y] - (operated - weight_of(mask_ref, x, y) * beside)


def later_sweep_kernel(
    anchor_ref, count_ref, mask_ref, pre_ref, field_ref,
    above_ref, below_ref, left_ref, right_ref, inv_hbm, out_ref, inv_ref, sem, packed_ref,
):
    rows, columns = field_ref.shape[:2]
    fetch_inverse(count_ref, inv_hbm, inv_ref, sem)
    for x in range(rows):
        for y in range(columns):
            outside = []
            if x + 1 == rows:
                outside.append(below_ref[0, y])
            if x == 0:
                outside.append(above_ref[0, y])
            if y + 1 == columns:
                outside.append(right_ref[x, 0])
            if y == 0:
                outside.append(left_ref[x, 0])
            value = pre_ref[x, y]
            if outside:
                halo = outside[0].astype(jnp.float32)
                for term in outside[1:]:
                    halo = halo + term.astype(jnp.float32)
                value = value + weight_of(mask_ref, x, y) * halo
            packed_ref[x, y] = value.astype(jnp.bfloat16)
    out_ref[...] = field_ref[...]
    deposit_patches(anchor_ref, count_ref, packed_ref, inv_ref, out_ref)


SMEM = pl.BlockSpec(memory_space=pltpu.SMEM)
VMEM = pl.BlockSpec(memory_space=pltpu.VMEM)
ANY = pl.BlockSpec(memory_space=pl.ANY)


def first_sweep(src, inverse, anchors, count, mask):
    rows, columns, depth, loads = src.shape
    row_edge = jax.ShapeDtypeStruct((1, columns, depth, loads), jnp.bfloat16)
    column_edge = jax.ShapeDtypeStruct((rows, 1, depth, loads), jnp.bfloat16)
    return pl.pallas_call(
        first_sweep_kernel,
        out_shape=(
            jax.ShapeDtypeStruct(src.shape, jnp.float32),
            row_edge, row_edge, column_edge, column_edge,
        ),
        in_specs=[SMEM, SMEM, SMEM, VMEM, ANY],
        out_specs=(VMEM,) * 5,
        scratch_shapes=[
            pltpu.VMEM(inverse.shape, inverse.dtype),
            pltpu.SemaphoreType.DMA(()),
        ],
    )(anchors, count.reshape(1), mask, src, inverse)


def operator_part(load, field, operator, stiffness, mask):
    rows, columns, depth, loads = field.shape
    flops = 2 * rows * columns * depth * depth * loads * 6
    return pl.pallas_call(
        operator_kernel,
        out_shape=jax.ShapeDtypeStruct(field.shape, jnp.float32),
        in_specs=[SMEM, SMEM, VMEM, VMEM, VMEM],
        out_specs=VMEM,
        cost_estimate=pl.CostEstimate(
            flops=flops, bytes_accessed=3 * field.size * 4, transcendentals=0
        ),
    )(mask, stiffness, load, field, operator)


def later_sweep(pre, field, halos, inverse, anchors, count, mask):
    return pl.pallas_call(
        later_sweep_kernel,
        out_shape=jax.ShapeDtypeStruct(field.shape, jnp.float32),
        in_specs=[SMEM, SMEM, SMEM] + [VMEM] * 6 + [ANY],
        out_specs=VMEM,
        scratch_shapes=[
            pltpu.VMEM(inverse.shape, inverse.dtype),
            pltpu.SemaphoreType.DMA(()),
            pltpu.VMEM(field.shape, jnp.bfloat16),
        ],
    )(anchors, count.reshape(1), mask, pre, field, *halos, inverse)


def shifted_in(edge, axis, forward):
    count = lax.axis_size(axis)
    if forward:
        pairs = [(i, i + 1) for i in range(count - 1)]
    else:
        pairs = [(i + 1, i) for i in range(count - 1)]
    return lax.ppermute(edge, axis, pairs)


def per_device(
    load_field, stiffness, fault_mask, column_operator, patch_inverse, patch_anchor, patch_count
):
    inverse = patch_inverse[0, 0]
    anchors = patch_anchor[0, 0]
    count = patch_count[0, 0]

    field, top, bottom, left, right = first_sweep(load_field, inverse, anchors, count, fault_mask)
    if SWEEPS == 2:
        halos = (
            shifted_in(bottom, "gx", True),
            shifted_in(top, "gx", False),
            shifted_in(right, "gy", True),
            shifted_in(left, "gy", False),
        )
        pre = operator_part(load_field, field, column_operator, stiffness, fault_mask)
        field = later_sweep(pre, field, halos, inverse, anchors, count, fault_mask)
    return field


def solution(mesh):
    return jax.shard_map(
        per_device,
        mesh=mesh,
        in_specs=(
            P("gx", "gy", None, None),
            P("gx", "gy"),
            P("gx", "gy"),
            P(),
            P("gx", "gy", None, None, None),
            P("gx", "gy", None),
            P("gx", "gy"),
        ),
        out_specs=P("gx", "gy", None, None),
        check_vma=False,
    )
```

```python
import jax
import jax.numpy as jnp
from jax import lax
from jax.experimental import pallas as pl
from jax.experimental.pallas import tpu as pltpu
from jax.sharding import PartitionSpec as P

SWEEPS = 2


damping = 0.5


def weight_of(mask_ref, x, y):
    return 1.0 - 0.6 * mask_ref[x, y].astype(jnp.float32)


def deposit_patches(anchor_ref, count_ref, src_ref, inv_ref, acc_ref):
    rows, columns, depth, loads = src_ref.shape
    slots = inv_ref.shape[0]
    count = count_ref[0]
    for number in range(slots):

        @pl.when(number < count)
        def _():
            anchor = anchor_ref[number]
            row = anchor // (columns - 1)
            column = anchor % (columns - 1)
            pieces = [
                src_ref[row + i, column + j].astype(jnp.bfloat16)
                for i in range(2)
                for j in range(2)
            ]
            piece = jnp.concatenate(pieces, axis=0)
            term = damping * jnp.dot(
                inv_ref[number], piece, preferred_element_type=jnp.float32
            )
            for k in range(4):
                i, j = divmod(k, 2)
                acc_ref[row + i, column + j] += term[k * depth : (k + 1) * depth]


def first_sweep_kernel(
    anchor_ref, count_ref, mask_ref, src_ref, inv_ref,
    out_ref, top_ref, bottom_ref, left_ref, right_ref,
):
    rows, columns = src_ref.shape[:2]
    acc_ref = out_ref
    acc_ref[...] = jnp.zeros(acc_ref.shape, jnp.float32)
    deposit_patches(anchor_ref, count_ref, src_ref, inv_ref, acc_ref)
    for y in range(columns):
        top_ref[0, y] = (weight_of(mask_ref, 0, y) * acc_ref[0, y]).astype(top_ref.dtype)
        bottom_ref[0, y] = (weight_of(mask_ref, rows - 1, y) * acc_ref[rows - 1, y]).astype(bottom_ref.dtype)
    for x in range(rows):
        left_ref[x, 0] = (weight_of(mask_ref, x, 0) * acc_ref[x, 0]).astype(left_ref.dtype)
        right_ref[x, 0] = (weight_of(mask_ref, x, columns - 1) * acc_ref[x, columns - 1]).astype(right_ref.dtype)


def operator_kernel(mask_ref, stiffness_ref, load_ref, field_ref, operator_ref, pre_ref):
    rows, columns, depth, loads = field_ref.shape

    def weighted(x, y):
        return weight_of(mask_ref, x, y) * field_ref[x, y]

    for x in range(rows):
        wide = jnp.concatenate([field_ref[x, y] for y in range(columns)], axis=1)
        local = jnp.dot(
            operator_ref[...], wide,
            precision=lax.Precision.HIGHEST,
            preferred_element_type=jnp.float32,
        )
        for y in range(columns):
            near = [
                weighted(x + dx, y + dy)
                for dx, dy in ((1, 0), (-1, 0), (0, 1), (0, -1))
                if 0 <= x + dx < rows and 0 <= y + dy < columns
            ]
            beside = near[0]
            for term in near[1:]:
                beside = beside + term
            operated = stiffness_ref[x, y] * local[:, y * loads : (y + 1) * loads]
            pre_ref[x, y] = load_ref[x, y] - (operated - weight_of(mask_ref, x, y) * beside)


def later_sweep_kernel(
    anchor_ref, count_ref, mask_ref, pre_ref, field_ref, halo_ref, inv_ref, out_ref, packed_ref,
):
    rows, columns = field_ref.shape[:2]
    above_at, below_at = 0, columns
    left_at, right_at = 2 * columns, 2 * columns + rows
    for x in range(rows):
        for y in range(columns):
            outside = []
            if x + 1 == rows:
                outside.append(halo_ref[below_at + y])
            if x == 0:
                outside.append(halo_ref[above_at + y])
            if y + 1 == columns:
                outside.append(halo_ref[right_at + x])
            if y == 0:
                outside.append(halo_ref[left_at + x])
            value = pre_ref[x, y]
            if outside:
                halo = outside[0].astype(jnp.float32)
                for term in outside[1:]:
                    halo = halo + term.astype(jnp.float32)
                value = value + weight_of(mask_ref, x, y) * halo
            packed_ref[x, y] = value.astype(jnp.bfloat16)
    out_ref[...] = field_ref[...]
    deposit_patches(anchor_ref, count_ref, packed_ref, inv_ref, out_ref)


SMEM = pl.BlockSpec(memory_space=pltpu.SMEM)
VMEM = pl.BlockSpec(memory_space=pltpu.VMEM)


def first_sweep(src, inverse, anchors, count, mask):
    rows, columns, depth, loads = src.shape
    row_edge = jax.ShapeDtypeStruct((1, columns, depth, loads), jnp.bfloat16)
    column_edge = jax.ShapeDtypeStruct((rows, 1, depth, loads), jnp.bfloat16)
    return pl.pallas_call(
        first_sweep_kernel,
        out_shape=(
            jax.ShapeDtypeStruct(src.shape, jnp.float32),
            row_edge, row_edge, column_edge, column_edge,
        ),
        in_specs=[SMEM, SMEM, SMEM, VMEM, VMEM],
        out_specs=(VMEM,) * 5,
    )(anchors, count.reshape(1), mask, src, inverse)


def operator_part(load, field, operator, stiffness, mask):
    rows, columns, depth, loads = field.shape
    flops = 2 * rows * columns * depth * depth * loads * 6
    return pl.pallas_call(
        operator_kernel,
        out_shape=jax.ShapeDtypeStruct(field.shape, jnp.float32),
        in_specs=[SMEM, SMEM, VMEM, VMEM, VMEM],
        out_specs=VMEM,
        cost_estimate=pl.CostEstimate(
            flops=flops, bytes_accessed=3 * field.size * 4, transcendentals=0
        ),
    )(mask, stiffness, load, field, operator)


def later_sweep(pre, field, halos, inverse, anchors, count, mask):
    depth, loads = field.shape[2:]
    halo = jnp.concatenate([h.reshape(-1, depth, loads) for h in halos], axis=0)
    return pl.pallas_call(
        later_sweep_kernel,
        out_shape=jax.ShapeDtypeStruct(field.shape, jnp.float32),
        in_specs=[SMEM, SMEM, SMEM] + [VMEM] * 4,
        out_specs=VMEM,
        scratch_shapes=[pltpu.VMEM(field.shape, jnp.bfloat16)],
    )(anchors, count.reshape(1), mask, pre, field, halo, inverse)


def shifted_in(edge, axis, forward):
    count = lax.axis_size(axis)
    if forward:
        pairs = [(i, i + 1) for i in range(count - 1)]
    else:
        pairs = [(i + 1, i) for i in range(count - 1)]
    return lax.ppermute(edge, axis, pairs)


def per_device(
    load_field, stiffness, fault_mask, column_operator, patch_inverse, patch_anchor, patch_count
):
    inverse = patch_inverse[0, 0]
    anchors = patch_anchor[0, 0]
    count = patch_count[0, 0]

    field, top, bottom, left, right = first_sweep(load_field, inverse, anchors, count, fault_mask)
    if SWEEPS == 2:
        halos = (
            shifted_in(bottom, "gx", True),
            shifted_in(top, "gx", False),
            shifted_in(right, "gy", True),
            shifted_in(left, "gy", False),
        )
        pre = operator_part(load_field, field, column_operator, stiffness, fault_mask)
        field = later_sweep(pre, field, halos, inverse, anchors, count, fault_mask)
    return field


def solution(mesh):
    return jax.shard_map(
        per_device,
        mesh=mesh,
        in_specs=(
            P("gx", "gy", None, None),
            P("gx", "gy"),
            P("gx", "gy"),
            P(),
            P("gx", "gy", None, None, None),
            P("gx", "gy", None),
            P("gx", "gy"),
        ),
        out_specs=P("gx", "gy", None, None),
        check_vma=False,
    )
```

```python
import jax
import jax.numpy as jnp
from jax import lax
from jax.experimental import pallas as pl
from jax.experimental.pallas import tpu as pltpu
from jax.sharding import PartitionSpec as P

SWEEPS = 2


damping = 0.5


def weight_of(mask_ref, x, y):
    return 1.0 - 0.6 * mask_ref[x, y].astype(jnp.float32)


def deposit_patches(anchor_ref, count_ref, src_ref, inv_ref, acc_ref):
    rows, columns, depth, loads = src_ref.shape
    slots = inv_ref.shape[0]
    count = count_ref[0]
    for number in range(slots):

        @pl.when(number < count)
        def _():
            anchor = anchor_ref[number]
            row = anchor // (columns - 1)
            column = anchor % (columns - 1)
            pieces = [
                src_ref[row + i, column + j].astype(jnp.bfloat16)
                for i in range(2)
                for j in range(2)
            ]
            piece = jnp.concatenate(pieces, axis=0)
            term = damping * jnp.dot(
                inv_ref[number], piece, preferred_element_type=jnp.float32
            )
            for k in range(4):
                i, j = divmod(k, 2)
                acc_ref[row + i, column + j] += term[k * depth : (k + 1) * depth]


def first_sweep_kernel(
    anchor_ref, count_ref, mask_ref, src_ref, inv_ref,
    out_ref, top_ref, bottom_ref, left_ref, right_ref,
):
    rows, columns = src_ref.shape[:2]
    acc_ref = out_ref
    acc_ref[...] = jnp.zeros(acc_ref.shape, jnp.float32)
    deposit_patches(anchor_ref, count_ref, src_ref, inv_ref, acc_ref)
    for y in range(columns):
        top_ref[0, y] = (weight_of(mask_ref, 0, y) * acc_ref[0, y]).astype(top_ref.dtype)
        bottom_ref[0, y] = (weight_of(mask_ref, rows - 1, y) * acc_ref[rows - 1, y]).astype(bottom_ref.dtype)
    for x in range(rows):
        left_ref[x, 0] = (weight_of(mask_ref, x, 0) * acc_ref[x, 0]).astype(left_ref.dtype)
        right_ref[x, 0] = (weight_of(mask_ref, x, columns - 1) * acc_ref[x, columns - 1]).astype(right_ref.dtype)


def operator_kernel(mask_ref, stiffness_ref, load_ref, field_ref, operator_ref, pre_ref):
    rows, columns, depth, loads = field_ref.shape

    def weighted(x, y):
        return weight_of(mask_ref, x, y) * field_ref[x, y]

    for x in range(rows):
        wide = jnp.concatenate([field_ref[x, y] for y in range(columns)], axis=1)
        local = jnp.dot(
            operator_ref[...], wide,
            precision=lax.Precision.HIGHEST,
            preferred_element_type=jnp.float32,
        )
        for y in range(columns):
            near = [
                weighted(x + dx, y + dy)
                for dx, dy in ((1, 0), (-1, 0), (0, 1), (0, -1))
                if 0 <= x + dx < rows and 0 <= y + dy < columns
            ]
            beside = near[0]
            for term in near[1:]:
                beside = beside + term
            operated = stiffness_ref[x, y] * local[:, y * loads : (y + 1) * loads]
            pre_ref[x, y] = load_ref[x, y] - (operated - weight_of(mask_ref, x, y) * beside)


def later_sweep_kernel(
    anchor_ref, count_ref, mask_ref, pre_ref, field_ref,
    above_ref, below_ref, left_ref, right_ref, inv_ref, out_ref, packed_ref, cover_ref,
):
    rows, columns = field_ref.shape[:2]
    count = count_ref[0]
    for vertex in range(rows * columns):
        cover_ref[vertex] = 0
    for number in range(inv_ref.shape[0]):

        @pl.when(number < count)
        def _():
            anchor = anchor_ref[number]
            corner = (anchor // (columns - 1)) * columns + anchor % (columns - 1)
            for offset in (0, 1, columns, columns + 1):
                cover_ref[corner + offset] = 1

    for x in range(rows):
        for y in range(columns):
            pack_vertex(x, y, cover_ref, mask_ref, pre_ref, above_ref, below_ref,
                        left_ref, right_ref, packed_ref)
    out_ref[...] = field_ref[...]
    deposit_patches(anchor_ref, count_ref, packed_ref, inv_ref, out_ref)


def pack_vertex(x, y, cover_ref, mask_ref, pre_ref, above_ref, below_ref, left_ref,
                right_ref, packed_ref):
    rows, columns = pre_ref.shape[:2]

    @pl.when(cover_ref[x * columns + y] > 0)
    def _():
            outside = []
            if x + 1 == rows:
                outside.append(below_ref[0, y])
            if x == 0:
                outside.append(above_ref[0, y])
            if y + 1 == columns:
                outside.append(right_ref[x, 0])
            if y == 0:
                outside.append(left_ref[x, 0])
            value = pre_ref[x, y]
            if outside:
                halo = outside[0].astype(jnp.float32)
                for term in outside[1:]:
                    halo = halo + term.astype(jnp.float32)
                value = value + weight_of(mask_ref, x, y) * halo
            packed_ref[x, y] = value.astype(jnp.bfloat16)


SMEM = pl.BlockSpec(memory_space=pltpu.SMEM)
VMEM = pl.BlockSpec(memory_space=pltpu.VMEM)


def first_sweep(src, inverse, anchors, count, mask):
    rows, columns, depth, loads = src.shape
    row_edge = jax.ShapeDtypeStruct((1, columns, depth, loads), jnp.bfloat16)
    column_edge = jax.ShapeDtypeStruct((rows, 1, depth, loads), jnp.bfloat16)
    return pl.pallas_call(
        first_sweep_kernel,
        out_shape=(
            jax.ShapeDtypeStruct(src.shape, jnp.float32),
            row_edge, row_edge, column_edge, column_edge,
        ),
        in_specs=[SMEM, SMEM, SMEM, VMEM, VMEM],
        out_specs=(VMEM,) * 5,
    )(anchors, count.reshape(1), mask, src, inverse)


def operator_part(load, field, operator, stiffness, mask):
    rows, columns, depth, loads = field.shape
    flops = 2 * rows * columns * depth * depth * loads * 6
    return pl.pallas_call(
        operator_kernel,
        out_shape=jax.ShapeDtypeStruct(field.shape, jnp.float32),
        in_specs=[SMEM, SMEM, VMEM, VMEM, VMEM],
        out_specs=VMEM,
        cost_estimate=pl.CostEstimate(
            flops=flops, bytes_accessed=3 * field.size * 4, transcendentals=0
        ),
    )(mask, stiffness, load, field, operator)


def later_sweep(pre, field, halos, inverse, anchors, count, mask):
    return pl.pallas_call(
        later_sweep_kernel,
        out_shape=jax.ShapeDtypeStruct(field.shape, jnp.float32),
        in_specs=[SMEM, SMEM, SMEM] + [VMEM] * 7,
        out_specs=VMEM,
        scratch_shapes=[
            pltpu.VMEM(field.shape, jnp.bfloat16),
            pltpu.SMEM((field.shape[0] * field.shape[1],), jnp.int32),
        ],
    )(anchors, count.reshape(1), mask, pre, field, *halos, inverse)


def shifted_in(edge, axis, forward):
    count = lax.axis_size(axis)
    if forward:
        pairs = [(i, i + 1) for i in range(count - 1)]
    else:
        pairs = [(i + 1, i) for i in range(count - 1)]
    return lax.ppermute(edge, axis, pairs)


def per_device(
    load_field, stiffness, fault_mask, column_operator, patch_inverse, patch_anchor, patch_count
):
    inverse = patch_inverse[0, 0]
    anchors = patch_anchor[0, 0]
    count = patch_count[0, 0]

    field, top, bottom, left, right = first_sweep(load_field, inverse, anchors, count, fault_mask)
    if SWEEPS == 2:
        halos = (
            shifted_in(bottom, "gx", True),
            shifted_in(top, "gx", False),
            shifted_in(right, "gy", True),
            shifted_in(left, "gy", False),
        )
        pre = operator_part(load_field, field, column_operator, stiffness, fault_mask)
        field = later_sweep(pre, field, halos, inverse, anchors, count, fault_mask)
    return field


def solution(mesh):
    return jax.shard_map(
        per_device,
        mesh=mesh,
        in_specs=(
            P("gx", "gy", None, None),
            P("gx", "gy"),
            P("gx", "gy"),
            P(),
            P("gx", "gy", None, None, None),
            P("gx", "gy", None),
            P("gx", "gy"),
        ),
        out_specs=P("gx", "gy", None, None),
        check_vma=False,
    )
```

```python
import jax
import jax.numpy as jnp
from jax import lax
from jax.experimental import pallas as pl
from jax.experimental.pallas import tpu as pltpu
from jax.sharding import PartitionSpec as P

SWEEPS = 2


damping = 0.5


def weight_of(mask_ref, x, y):
    return 1.0 - 0.6 * mask_ref[x, y].astype(jnp.float32)


def deposit_patches(anchor_ref, count_ref, src_ref, inv_ref, acc_ref, inner=None):
    rows, columns, depth, loads = src_ref.shape
    slots = inv_ref.shape[0]
    count = count_ref[0]
    for number in range(slots):
        anchor = anchor_ref[number]
        row = anchor // (columns - 1)
        column = anchor % (columns - 1)
        take = number < count
        if inner is not None:
            interior = (row > 0) & (row + 2 < rows) & (column > 0) & (column + 2 < columns)
            take = take & (interior == inner)

        @pl.when(take)
        def _():
            pieces = [
                src_ref[row + i, column + j].astype(jnp.bfloat16)
                for i in range(2)
                for j in range(2)
            ]
            piece = jnp.concatenate(pieces, axis=0)
            term = damping * jnp.dot(
                inv_ref[number], piece, preferred_element_type=jnp.float32
            )
            for k in range(4):
                i, j = divmod(k, 2)
                acc_ref[row + i, column + j] += term[k * depth : (k + 1) * depth]


def first_sweep_kernel(
    anchor_ref, count_ref, mask_ref, src_ref, inv_ref,
    out_ref, top_ref, bottom_ref, left_ref, right_ref,
):
    rows, columns = src_ref.shape[:2]
    acc_ref = out_ref
    acc_ref[...] = jnp.zeros(acc_ref.shape, jnp.float32)
    deposit_patches(anchor_ref, count_ref, src_ref, inv_ref, acc_ref)
    for y in range(columns):
        top_ref[0, y] = (weight_of(mask_ref, 0, y) * acc_ref[0, y]).astype(top_ref.dtype)
        bottom_ref[0, y] = (weight_of(mask_ref, rows - 1, y) * acc_ref[rows - 1, y]).astype(bottom_ref.dtype)
    for x in range(rows):
        left_ref[x, 0] = (weight_of(mask_ref, x, 0) * acc_ref[x, 0]).astype(left_ref.dtype)
        right_ref[x, 0] = (weight_of(mask_ref, x, columns - 1) * acc_ref[x, columns - 1]).astype(right_ref.dtype)


def operator_kernel(
    anchor_ref, count_ref, mask_ref, stiffness_ref, load_ref, field_ref, operator_ref, inv_ref,
    pre_ref, base_ref, packed_ref,
):
    rows, columns, depth, loads = field_ref.shape

    def weighted(x, y):
        return weight_of(mask_ref, x, y) * field_ref[x, y]

    for x in range(rows):
        wide = jnp.concatenate([field_ref[x, y] for y in range(columns)], axis=1)
        local = jnp.dot(
            operator_ref[...], wide,
            precision=lax.Precision.HIGHEST,
            preferred_element_type=jnp.float32,
        )
        for y in range(columns):
            near = [
                weighted(x + dx, y + dy)
                for dx, dy in ((1, 0), (-1, 0), (0, 1), (0, -1))
                if 0 <= x + dx < rows and 0 <= y + dy < columns
            ]
            beside = near[0]
            for term in near[1:]:
                beside = beside + term
            operated = stiffness_ref[x, y] * local[:, y * loads : (y + 1) * loads]
            pre_ref[x, y] = load_ref[x, y] - (operated - weight_of(mask_ref, x, y) * beside)
            packed_ref[x, y] = pre_ref[x, y].astype(jnp.bfloat16)
    base_ref[...] = field_ref[...]
    deposit_patches(anchor_ref, count_ref, packed_ref, inv_ref, base_ref, inner=True)


def later_sweep_kernel(
    anchor_ref, count_ref, mask_ref, pre_ref, field_ref,
    above_ref, below_ref, left_ref, right_ref, inv_ref, out_ref, packed_ref,
):
    rows, columns = field_ref.shape[:2]
    for x in range(rows):
        for y in range(columns):
            outside = []
            if x + 1 == rows:
                outside.append(below_ref[0, y])
            if x == 0:
                outside.append(above_ref[0, y])
            if y + 1 == columns:
                outside.append(right_ref[x, 0])
            if y == 0:
                outside.append(left_ref[x, 0])
            value = pre_ref[x, y]
            if outside:
                halo = outside[0].astype(jnp.float32)
                for term in outside[1:]:
                    halo = halo + term.astype(jnp.float32)
                value = value + weight_of(mask_ref, x, y) * halo
            packed_ref[x, y] = value.astype(jnp.bfloat16)
    out_ref[...] = field_ref[...]
    deposit_patches(anchor_ref, count_ref, packed_ref, inv_ref, out_ref, inner=False)


SMEM = pl.BlockSpec(memory_space=pltpu.SMEM)
VMEM = pl.BlockSpec(memory_space=pltpu.VMEM)


def first_sweep(src, inverse, anchors, count, mask):
    rows, columns, depth, loads = src.shape
    row_edge = jax.ShapeDtypeStruct((1, columns, depth, loads), jnp.bfloat16)
    column_edge = jax.ShapeDtypeStruct((rows, 1, depth, loads), jnp.bfloat16)
    return pl.pallas_call(
        first_sweep_kernel,
        out_shape=(
            jax.ShapeDtypeStruct(src.shape, jnp.float32),
            row_edge, row_edge, column_edge, column_edge,
        ),
        in_specs=[SMEM, SMEM, SMEM, VMEM, VMEM],
        out_specs=(VMEM,) * 5,
    )(anchors, count.reshape(1), mask, src, inverse)


def operator_part(load, field, operator, stiffness, mask, inverse, anchors, count):
    rows, columns, depth, loads = field.shape
    flops = 2 * rows * columns * depth * depth * loads * 6
    return pl.pallas_call(
        operator_kernel,
        out_shape=(
            jax.ShapeDtypeStruct(field.shape, jnp.float32),
            jax.ShapeDtypeStruct(field.shape, jnp.float32),
        ),
        in_specs=[SMEM, SMEM, SMEM, SMEM, VMEM, VMEM, VMEM, VMEM],
        out_specs=(VMEM, VMEM),
        scratch_shapes=[pltpu.VMEM(field.shape, jnp.bfloat16)],
        cost_estimate=pl.CostEstimate(
            flops=flops, bytes_accessed=3 * field.size * 4, transcendentals=0
        ),
    )(anchors, count.reshape(1), mask, stiffness, load, field, operator, inverse)


def later_sweep(pre, field, halos, inverse, anchors, count, mask):
    return pl.pallas_call(
        later_sweep_kernel,
        out_shape=jax.ShapeDtypeStruct(field.shape, jnp.float32),
        in_specs=[SMEM, SMEM, SMEM] + [VMEM] * 7,
        out_specs=VMEM,
        scratch_shapes=[pltpu.VMEM(field.shape, jnp.bfloat16)],
    )(anchors, count.reshape(1), mask, pre, field, *halos, inverse)


def shifted_in(edge, axis, forward):
    count = lax.axis_size(axis)
    if forward:
        pairs = [(i, i + 1) for i in range(count - 1)]
    else:
        pairs = [(i + 1, i) for i in range(count - 1)]
    return lax.ppermute(edge, axis, pairs)


def per_device(
    load_field, stiffness, fault_mask, column_operator, patch_inverse, patch_anchor, patch_count
):
    inverse = patch_inverse[0, 0]
    anchors = patch_anchor[0, 0]
    count = patch_count[0, 0]

    field, top, bottom, left, right = first_sweep(load_field, inverse, anchors, count, fault_mask)
    if SWEEPS == 2:
        halos = (
            shifted_in(bottom, "gx", True),
            shifted_in(top, "gx", False),
            shifted_in(right, "gy", True),
            shifted_in(left, "gy", False),
        )
        pre, base = operator_part(
            load_field, field, column_operator, stiffness, fault_mask, inverse, anchors, count
        )
        field = later_sweep(pre, base, halos, inverse, anchors, count, fault_mask)
    return field


def solution(mesh):
    return jax.shard_map(
        per_device,
        mesh=mesh,
        in_specs=(
            P("gx", "gy", None, None),
            P("gx", "gy"),
            P("gx", "gy"),
            P(),
            P("gx", "gy", None, None, None),
            P("gx", "gy", None),
            P("gx", "gy"),
        ),
        out_specs=P("gx", "gy", None, None),
        check_vma=False,
    )
```
